128 devices in a mesh: ctx: 8 (over y_lo, z), fsdp: 16 (over y_hi, x, core).
Axes of the slice: x: 4, y: 4 (y_hi: 2, y_lo: 2; y = y_hi * 2 + y_lo), z: 4, core: 2. Of those that a mesh axis runs over, the one named last changes fastest.
Arguments:
- hidden: bfloat16 [16384, 16384], P('ctx', 'fsdp'), may hold values from -48 to 48
- w_query: bfloat16 [16384, 2048], P('fsdp'), may hold values from -0.0625 to 0.0625
- w_key_value: bfloat16 [16384, 256], P('fsdp'), may hold values from -0.046875 to 0.046875
- block_doc: int32 [32], replicated, may hold values from 0 to 7, never falling along the last dimension, each value on 1 to 16 neighbouring positions
Outputs:
- attended: bfloat16 [16384, 2048], P('ctx', 'fsdp')
The draws below stay inside these ranges and needn't reach their ends.
Inputs may be any that keep to these rules, and one draw needn't show every extreme that they name: `block_doc`: document ids never fall along the context; each document covers 1 to 16 blocks, one exactly 16.
All inputs are finite; a program needn't handle non-finite values.
Results may differ from the reference program's by a relative error of at most 0.01.
The reference program's roundings to bfloat16 on the way (of `q_rot`) count: a program that leaves them out, or rounds other values in their place, can miss the bound.
Values may be sent and summed in bfloat16 or wider, within the bound.
No kernel may reach another device: no remote copies, remote signals or barrier semaphores. Data moves between devices by JAX's collectives and lax.ppermute only.
A program may use at most 384 MiB of HBM per device.

```python
import math
import jax
import jax.numpy as jnp
import numpy as np
from jax import lax

D = 16384
DH = 128
HQ = 16
BLOCK = 512
TOK_DEV = 2048
TOKENS = 16384
NBLK = 32
DOCS = 8
N_CTX = 8


def draw_hidden(key, part):
    normals = jnp.clip(jax.random.normal(jax.random.fold_in(key, 11), (TOKENS, D), jnp.float32), -6.0, 6.0)
    return normals.astype(jnp.bfloat16)


def strengthened(drawn, key, source, target, blocks, factor):
    owner, partner = [(jnp.arange(drawn.shape[position]) // (drawn.shape[position] // blocks)).reshape([-1 if axis == position else 1 for axis in range(drawn.ndim)]) for position in (source, target)]
    chosen = jax.random.permutation(key, blocks)[partner]
    strong = (owner == chosen) | (owner == (partner + blocks // 2) % blocks)
    return jnp.where(strong, factor * drawn, drawn)


def steps_of(key, shape, pieces, smallest, high):
    factor_of, own = 1.0, jax.random.fold_in(key, 6)
    for position, blocks in pieces:
        steps = jnp.exp(jax.random.uniform(jax.random.fold_in(own, position), (blocks,), jnp.float32, smallest / len(pieces), high / len(pieces)))
        factor_of = factor_of * jnp.repeat(steps, shape[position] // blocks).reshape([-1 if axis == position else 1 for axis in range(len(shape))])
    return factor_of


def length_profile(amount, total, most, skew):
    weights = [(1 << 20) // math.isqrt(rank ** skew) + 1 for rank in range(2, amount + 1)]
    rest, given = total - most - (amount - 1), [1] * (amount - 1)
    while rest > 0:
        movable = [i for i in range(amount - 1) if given[i] < most]
        pool, budget = sum([weights[i] for i in movable]), rest
        for i in movable:
            more = min(most - given[i], max(1, budget * weights[i] // pool), rest)
            given[i] = given[i] + more
            rest = rest - more
    return np.array([most] + given)


def ragged_sizes(key, count, total, reach, lean):
    if count == 2:
        one = jax.random.randint(key, (), max(1, total - reach), min(reach, total - 1) + 1)
        return jnp.stack([one, total - one])
    lengths = jnp.asarray(length_profile(count, total, reach, lean), jnp.int32)
    pairs = (count - 1) // 2
    source_of, taker = lengths[1:1 + 2 * pairs:2], lengths[2:2 + 2 * pairs:2]
    slack = jnp.minimum(source_of - 1, reach - taker)
    passed = jax.random.randint(jax.random.fold_in(key, 1), (pairs,), 0, 1 << 20) % (slack + 1)
    lengths = lengths.at[1:1 + 2 * pairs:2].set(source_of - passed).at[2:2 + 2 * pairs:2].set(taker + passed)
    return lengths[jax.random.permutation(jax.random.fold_in(key, 2), count)]


def gaussian(key, extent, scale, bound, pieces=(), held_as=jnp.bfloat16):
    result = jax.random.normal(key, extent, jnp.float32) * scale
    if len(pieces) > 0:
        result = steps_of(key, extent, pieces, -0.22, 0.18) * result
    return jnp.clip(result, min=-bound, max=bound).astype(held_as)


def heavy_noise(stream_key, shape, width, most, pieces, heavy, held_as=jnp.bfloat16):
    entries = width * jax.random.normal(stream_key, shape, jnp.float32)
    if pieces:
        entries = entries * steps_of(stream_key, shape, pieces, -0.22, 0.18)
    return jnp.clip(strengthened(entries, jax.random.fold_in(stream_key, 3), *heavy), -most, most).astype(held_as)


def setup_inputs(seed: int = 0) -> dict:
    streams_of = jax.random.split(jax.random.key(seed), 5)
    hidden = draw_hidden(jax.random.fold_in(streams_of[4], 71), 0)
    w_query = heavy_noise(streams_of[1], (D, HQ * DH), D ** -0.5, 0.0625, ((0, 16),), (0, 1, 16, 2.0))
    w_key_value = gaussian(streams_of[2], (D, 2 * DH), D ** -0.5, 0.046875, ((0, 16),))
    block_doc = jnp.searchsorted(jnp.cumsum(ragged_sizes(streams_of[3], DOCS, NBLK, NBLK // 2, 0)), jnp.arange(NBLK), side="right").astype(jnp.int32)
    return {"hidden": hidden, "w_query": w_query, "w_key_value": w_key_value, "block_doc": block_doc}


masked_low = -1.0e30


def rotate_pairs(vectors, positions):
    half_dim = DH // 2
    frequency = 500000.0 ** (-2.0 * jnp.arange(half_dim, dtype=jnp.float32) / DH)
    angles = positions[:, None].astype(jnp.float32) * frequency[None, :]
    cosine = jnp.cos(angles)
    sine = jnp.sin(angles)
    first_half = vectors[..., :half_dim]
    second_half = vectors[..., half_dim:]
    return jnp.concatenate([first_half * cosine - second_half * sine, second_half * cosine + first_half * sine], -1)


def reference(hidden, w_query, w_key_value, block_doc):
    query = jnp.dot(hidden, w_query, preferred_element_type=jnp.float32)
    key_val = jnp.dot(hidden, w_key_value, preferred_element_type=jnp.float32)
    positions = jnp.arange(TOKENS, dtype=jnp.int32)
    keys = rotate_pairs(key_val[:, :DH], positions).astype(jnp.bfloat16)
    values = key_val[:, DH:].astype(jnp.bfloat16)
    heads = jnp.transpose(query.reshape(TOKENS, HQ, DH), (1, 0, 2))
    q_rot = rotate_pairs(heads, positions).astype(jnp.bfloat16)
    token_doc = jnp.repeat(block_doc, BLOCK)
    scale = DH ** -0.5
    block_starts = jnp.arange(N_CTX, dtype=jnp.int32) * TOK_DEV

    def one_head(query_head):
        query_blocks = query_head.reshape(N_CTX, TOK_DEV, DH)

        def one_block(pair):
            query_rows, first_row = pair
            query_pos = first_row + jnp.arange(TOK_DEV, dtype=jnp.int32)
            query_doc = lax.dynamic_slice_in_dim(token_doc, first_row, TOK_DEV, 0)
            allowed = (positions[None, :] <= query_pos[:, None]) & (query_doc[:, None] == token_doc[None, :])
            scores = jnp.dot(query_rows, keys.T, preferred_element_type=jnp.float32) * scale
            scores = jnp.where(allowed, scores, masked_low)
            top = jnp.max(scores, axis=-1)
            weights = jnp.where(allowed, jnp.exp(scores - top[:, None]), 0.0)
            total = jnp.sum(weights, axis=-1)
            output = jnp.dot(weights.astype(jnp.bfloat16), values, preferred_element_type=jnp.float32)
            return (output / total[:, None]).astype(jnp.bfloat16)

        return lax.map(one_block, (query_blocks, block_starts)).reshape(TOKENS, DH)

    outputs = lax.map(one_head, q_rot)
    return jnp.transpose(outputs, (1, 0, 2)).reshape(TOKENS, HQ * DH)
```

```python
import jax
import jax.numpy as jnp
from jax import lax
from jax.sharding import PartitionSpec as P

DH = 128
HQ = 16
BLOCK = 512
MAX_DOC_BLOCKS = 16


masked_low = -1e30


def frequencies():
    half_dim = DH // 2
    return 500000.0 ** (-2.0 * jnp.arange(half_dim, dtype=jnp.float32) / DH)


def rotate_pairs(vectors, positions):
    half_dim = DH // 2
    angles = positions[:, None].astype(jnp.float32) * frequencies()[None, :]
    cosine = jnp.cos(angles)
    sine = jnp.sin(angles)
    first_half = vectors[..., :half_dim]
    second_half = vectors[..., half_dim:]
    return jnp.concatenate(
        [first_half * cosine - second_half * sine, second_half * cosine + first_half * sine], -1
    )


def document_of(positions, block_doc):
    block_ids = positions // BLOCK
    table_ids = jnp.arange(block_doc.shape[0], dtype=jnp.int32)
    matches = block_ids[:, None] == table_ids[None, :]
    return jnp.sum(jnp.where(matches, block_doc[None, :], 0), axis=1)


def attend_tile(state_in, query_rows, query_pos, query_doc, key_rows, value_rows, key_pos, key_doc, valid):
    allowed = (key_pos[None, :] <= query_pos[:, None]) & (query_doc[:, None] == key_doc[None, :]) & valid
    scale = DH ** (-0.5)
    run_max, run_sum, run_out = state_in
    scores = (
        jnp.einsum("hqe,ke->hqk", query_rows, key_rows, preferred_element_type=jnp.float32) * scale
    )
    scores = jnp.where(allowed[None], scores, masked_low)
    new_max = jnp.maximum(run_max, jnp.max(scores, axis=-1))
    weights_f = jnp.where(allowed[None], jnp.exp(scores - new_max[..., None]), 0.0)
    rescale = jnp.exp(run_max - new_max)
    new_sum = run_sum * rescale + jnp.sum(weights_f, axis=-1)
    new_out = run_out * rescale[..., None] + jnp.einsum(
        "hqk,ke->hqe",
        weights_f.astype(jnp.bfloat16),
        value_rows,
        preferred_element_type=jnp.float32,
    )
    return (new_max, new_sum, new_out)


def gather_fsdp(piece, n_fsdp):
    me = lax.axis_index("fsdp")
    bits = n_fsdp.bit_length() - 1
    held = piece
    for bit in reversed(range(bits)):
        pairs = [(i, i ^ (1 << bit)) for i in range(n_fsdp)]
        theirs = lax.ppermute(held, "fsdp", pairs)
        mine_first = ((me >> bit) & 1) == 0
        held = jnp.where(mine_first, jnp.stack([held, theirs]), jnp.stack([theirs, held]))
    held = jnp.transpose(held, tuple(reversed(range(bits))) + tuple(range(bits, held.ndim)))
    return held.reshape((n_fsdp,) + piece.shape)


def on_device(hidden, w_query, w_key_value, block_doc):
    tok_rows, feat_rows = hidden.shape
    n_fsdp = lax.axis_size("fsdp")
    n_ctx = lax.axis_size("ctx")
    quarter = DH // 2 // n_fsdp
    eighth = DH // n_fsdp
    w_keys = w_key_value[:, :DH]
    w_comb = jnp.concatenate(
        [
            w_query.reshape(feat_rows, n_fsdp, DH),
            w_keys[:, : DH // 2].reshape(feat_rows, n_fsdp, quarter),
            w_keys[:, DH // 2 :].reshape(feat_rows, n_fsdp, quarter),
            w_key_value[:, DH:].reshape(feat_rows, n_fsdp, eighth),
        ],
        axis=2,
    )
    reduced = lax.psum_scatter(
        jnp.einsum("td,dfc->ftc", hidden, w_comb, preferred_element_type=jnp.float32),
        "fsdp",
        scatter_dimension=0,
        tiled=True,
    )[0]
    me = lax.axis_index("ctx")
    me_f = lax.axis_index("fsdp")
    local_range = jnp.arange(tok_rows, dtype=jnp.int32)
    positions = me * tok_rows + local_range
    query = reduced[None, :, :DH]
    q_rot = rotate_pairs(query, positions).astype(jnp.bfloat16)
    key_a = reduced[:, DH : DH + quarter]
    key_b = reduced[:, DH + quarter : DH + 2 * quarter]
    vals = reduced[:, DH + 2 * quarter :]
    freq = lax.dynamic_slice_in_dim(frequencies(), me_f * quarter, quarter)
    angles = positions[:, None].astype(jnp.float32) * freq[None, :]
    cosine = jnp.cos(angles)
    sine = jnp.sin(angles)
    piece = jnp.concatenate(
        [key_a * cosine - key_b * sine, key_b * cosine + key_a * sine, vals], axis=1
    ).astype(jnp.bfloat16)
    gathered = gather_fsdp(piece, n_fsdp)
    gathered = jnp.transpose(gathered, (1, 0, 2))
    kv = jnp.concatenate(
        [
            gathered[:, :, :quarter].reshape(tok_rows, DH // 2),
            gathered[:, :, quarter : 2 * quarter].reshape(tok_rows, DH // 2),
            gathered[:, :, 2 * quarter :].reshape(tok_rows, DH),
        ],
        axis=1,
    )

    query_doc = document_of(positions, block_doc)
    reach = min((MAX_DOC_BLOCKS * BLOCK - 1 + tok_rows - 1) // tok_rows, n_ctx - 1)
    heads_dev = 1
    state = (
        jnp.full((heads_dev, tok_rows), masked_low, jnp.float32),
        jnp.zeros((heads_dev, tok_rows), jnp.float32),
        jnp.zeros((heads_dev, tok_rows, DH), jnp.float32),
    )
    for back in range(reach + 1):
        if back == 0:
            kv_here = kv
        else:
            kv_here = lax.ppermute(kv, "ctx", [(j, j + back) for j in range(n_ctx - back)])
        owner = me - back
        key_pos = owner * tok_rows + local_range
        key_doc = document_of(key_pos, block_doc)
        state = attend_tile(
            state, q_rot, positions, query_doc, kv_here[:, :DH], kv_here[:, DH:], key_pos, key_doc,
            owner >= 0,
        )
    run_max, run_sum, run_out = state
    attended = (run_out / run_sum[..., None]).astype(jnp.bfloat16)
    return jnp.transpose(attended, (1, 0, 2)).reshape(tok_rows, heads_dev * DH)


def solution(mesh):
    return jax.shard_map(
        on_device,
        mesh=mesh,
        in_specs=(P("ctx", "fsdp"), P("fsdp", None), P("fsdp", None), P()),
        out_specs=P("ctx", "fsdp"),
        check_vma=False,
    )
```

```python
import functools

import jax
import jax.numpy as jnp
from jax import lax
from jax.experimental import pallas as pl
from jax.experimental.pallas import tpu as pltpu
from jax.sharding import PartitionSpec as P

DH = 128
HQ = 16
BLOCK = 512
MAX_DOC_BLOCKS = 16


masked_low = -1e30


def frequencies():
    half_dim = DH // 2
    return 500000.0 ** (-2.0 * jnp.arange(half_dim, dtype=jnp.float32) / DH)


def rotate_pairs(vectors, positions):
    half_dim = DH // 2
    angles = positions[:, None].astype(jnp.float32) * frequencies()[None, :]
    cosine = jnp.cos(angles)
    sine = jnp.sin(angles)
    first_half = vectors[..., :half_dim]
    second_half = vectors[..., half_dim:]
    return jnp.concatenate(
        [first_half * cosine - second_half * sine, second_half * cosine + first_half * sine], -1
    )


def document_of(positions, block_doc):
    block_ids = positions // BLOCK
    table_ids = jnp.arange(block_doc.shape[0], dtype=jnp.int32)
    matches = block_ids[:, None] == table_ids[None, :]
    return jnp.sum(jnp.where(matches, block_doc[None, :], 0), axis=1)


def attend_tile(state_in, query_rows, query_pos, query_doc, key_rows, value_rows, key_pos, key_doc, valid):
    allowed = (key_pos[None, :] <= query_pos[:, None]) & (query_doc[:, None] == key_doc[None, :]) & valid
    scale = DH ** (-0.5)
    run_max, run_sum, run_out = state_in
    scores = (
        jnp.einsum("hqe,ke->hqk", query_rows, key_rows, preferred_element_type=jnp.float32) * scale
    )
    scores = jnp.where(allowed[None], scores, masked_low)
    new_max = jnp.maximum(run_max, jnp.max(scores, axis=-1))
    weights_f = jnp.where(allowed[None], jnp.exp(scores - new_max[..., None]), 0.0)
    rescale = jnp.exp(run_max - new_max)
    new_sum = run_sum * rescale + jnp.sum(weights_f, axis=-1)
    new_out = run_out * rescale[..., None] + jnp.einsum(
        "hqk,ke->hqe",
        weights_f.astype(jnp.bfloat16),
        value_rows,
        preferred_element_type=jnp.float32,
    )
    return (new_max, new_sum, new_out)


def flash_kernel(blocks_per_ctx, n_k, scalars, q_ref, k_ref, v_ref, o_ref, m_sc, l_sc, acc_sc):
    qi = pl.program_id(0)
    ki = pl.program_id(1)
    me = scalars[0]
    q_blk = me * blocks_per_ctx + qi
    k_blk = (me - ki // blocks_per_ctx) * blocks_per_ctx + ki % blocks_per_ctx
    q_doc = scalars[1 + q_blk]
    k_doc = scalars[1 + jnp.maximum(k_blk, 0)]
    needed = (k_blk >= 0) & (k_blk <= q_blk) & (k_doc == q_doc)

    @pl.when(ki == 0)
    def _():
        m_sc[...] = jnp.full(m_sc.shape, masked_low, jnp.float32)
        l_sc[...] = jnp.zeros(l_sc.shape, jnp.float32)
        acc_sc[...] = jnp.zeros(acc_sc.shape, jnp.float32)

    def update(diagonal):
        scale = DH ** (-0.5)
        scores = lax.dot_general(
            q_ref[...], k_ref[...], (((1,), (1,)), ((), ())), preferred_element_type=jnp.float32
        ) * scale
        if diagonal:
            rows = lax.broadcasted_iota(jnp.int32, scores.shape, 0)
            cols = lax.broadcasted_iota(jnp.int32, scores.shape, 1)
            allowed = cols <= rows
            scores = jnp.where(allowed, scores, masked_low)
        m_prev = m_sc[...]
        m_new = jnp.maximum(m_prev, jnp.max(scores, axis=1, keepdims=True))
        weights = jnp.exp(scores - m_new[:, :1])
        if diagonal:
            weights = jnp.where(allowed, weights, 0.0)
        rescale = jnp.exp(m_prev - m_new)
        l_sc[...] = l_sc[...] * rescale + jnp.sum(weights, axis=1, keepdims=True)
        acc_sc[...] = acc_sc[...] * rescale + jnp.dot(
            weights.astype(jnp.bfloat16), v_ref[...], preferred_element_type=jnp.float32
        )
        m_sc[...] = m_new

    @pl.when(needed & (k_blk < q_blk))
    def _():
        update(False)

    @pl.when(needed & (k_blk == q_blk))
    def _():
        update(True)

    @pl.when(ki == n_k - 1)
    def _():
        o_ref[...] = (acc_sc[...] / l_sc[...]).astype(o_ref.dtype)


def flash_attend(me, block_doc, q_rot, kv_blocks):
    n_back, tok_rows, _ = kv_blocks.shape
    blocks_per_ctx = tok_rows // BLOCK
    n_q = blocks_per_ctx
    n_k = n_back * blocks_per_ctx
    scalars = jnp.concatenate([me.reshape(1).astype(jnp.int32), block_doc.astype(jnp.int32)])
    grid_spec = pltpu.PrefetchScalarGridSpec(
        num_scalar_prefetch=1,
        grid=(n_q, n_k),
        in_specs=[
            pl.BlockSpec((BLOCK, DH), lambda qi, ki, sc: (qi, 0)),
            pl.BlockSpec(
                (None, BLOCK, DH), lambda qi, ki, sc: (ki // blocks_per_ctx, ki % blocks_per_ctx, 0)
            ),
            pl.BlockSpec(
                (None, BLOCK, DH), lambda qi, ki, sc: (ki // blocks_per_ctx, ki % blocks_per_ctx, 1)
            ),
        ],
        out_specs=pl.BlockSpec((BLOCK, DH), lambda qi, ki, sc: (qi, 0)),
        scratch_shapes=[
            pltpu.VMEM((BLOCK, DH), jnp.float32),
            pltpu.VMEM((BLOCK, DH), jnp.float32),
            pltpu.VMEM((BLOCK, DH), jnp.float32),
        ],
    )
    return pl.pallas_call(
        functools.partial(flash_kernel, blocks_per_ctx, n_k),
        out_shape=jax.ShapeDtypeStruct((tok_rows, DH), jnp.bfloat16),
        grid_spec=grid_spec,
        compiler_params=pltpu.CompilerParams(dimension_semantics=("arbitrary", "arbitrary")),
        cost_estimate=pl.CostEstimate(
            flops=4 * tok_rows * tok_rows * DH * n_back // 2,
            transcendentals=tok_rows * tok_rows * n_back // 2,
            bytes_accessed=kv_blocks.size * 2 * n_q + 4 * tok_rows * DH,
        ),
    )(scalars, q_rot, kv_blocks, kv_blocks)


def gather_fsdp(piece, n_fsdp):
    me = lax.axis_index("fsdp")
    bits = n_fsdp.bit_length() - 1
    held = piece
    for bit in reversed(range(bits)):
        pairs = [(i, i ^ (1 << bit)) for i in range(n_fsdp)]
        theirs = lax.ppermute(held, "fsdp", pairs)
        mine_first = ((me >> bit) & 1) == 0
        held = jnp.where(mine_first, jnp.stack([held, theirs]), jnp.stack([theirs, held]))
    held = jnp.transpose(held, tuple(reversed(range(bits))) + tuple(range(bits, held.ndim)))
    return held.reshape((n_fsdp,) + piece.shape)


def on_device(hidden, w_query, w_key_value, block_doc):
    tok_rows, feat_rows = hidden.shape
    n_fsdp = lax.axis_size("fsdp")
    n_ctx = lax.axis_size("ctx")
    quarter = DH // 2 // n_fsdp
    eighth = DH // n_fsdp
    w_keys = w_key_value[:, :DH]
    w_comb = jnp.concatenate(
        [
            w_query.reshape(feat_rows, n_fsdp, DH),
            w_keys[:, : DH // 2].reshape(feat_rows, n_fsdp, quarter),
            w_keys[:, DH // 2 :].reshape(feat_rows, n_fsdp, quarter),
            w_key_value[:, DH:].reshape(feat_rows, n_fsdp, eighth),
        ],
        axis=2,
    )
    reduced = lax.psum_scatter(
        jnp.einsum("td,dfc->ftc", hidden, w_comb, preferred_element_type=jnp.float32),
        "fsdp",
        scatter_dimension=0,
        tiled=True,
    )[0]
    me = lax.axis_index("ctx")
    me_f = lax.axis_index("fsdp")
    local_range = jnp.arange(tok_rows, dtype=jnp.int32)
    positions = me * tok_rows + local_range
    query = reduced[None, :, :DH]
    q_rot = rotate_pairs(query, positions).astype(jnp.bfloat16)
    key_a = reduced[:, DH : DH + quarter]
    key_b = reduced[:, DH + quarter : DH + 2 * quarter]
    vals = reduced[:, DH + 2 * quarter :]
    freq = lax.dynamic_slice_in_dim(frequencies(), me_f * quarter, quarter)
    angles = positions[:, None].astype(jnp.float32) * freq[None, :]
    cosine = jnp.cos(angles)
    sine = jnp.sin(angles)
    piece = jnp.concatenate(
        [key_a * cosine - key_b * sine, key_b * cosine + key_a * sine, vals], axis=1
    ).astype(jnp.bfloat16)
    gathered = gather_fsdp(piece, n_fsdp)
    gathered = jnp.transpose(gathered, (1, 0, 2))
    kv = jnp.concatenate(
        [
            gathered[:, :, :quarter].reshape(tok_rows, DH // 2),
            gathered[:, :, quarter : 2 * quarter].reshape(tok_rows, DH // 2),
            gathered[:, :, 2 * quarter :].reshape(tok_rows, DH),
        ],
        axis=1,
    )

    reach = min((MAX_DOC_BLOCKS * BLOCK - 1 + tok_rows - 1) // tok_rows, n_ctx - 1)
    kv_blocks = [kv] + [
        lax.ppermute(kv, "ctx", [(j, j + back) for j in range(n_ctx - back)])
        for back in range(1, reach + 1)
    ]
    return flash_attend(me, block_doc, q_rot[0], jnp.stack(kv_blocks))


def solution(mesh):
    return jax.shard_map(
        on_device,
        mesh=mesh,
        in_specs=(P("ctx", "fsdp"), P("fsdp", None), P("fsdp", None), P()),
        out_specs=P("ctx", "fsdp"),
        check_vma=False,
    )
```

```python
import functools

import jax
import jax.numpy as jnp
from jax import lax
from jax.experimental import pallas as pl
from jax.experimental.pallas import tpu as pltpu
from jax.sharding import PartitionSpec as P

DH = 128
HQ = 16
BLOCK = 512
MAX_DOC_BLOCKS = 16


masked_low = -1e30


def frequencies():
    half_dim = DH // 2
    return 500000.0 ** (-2.0 * jnp.arange(half_dim, dtype=jnp.float32) / DH)


def rotate_pairs(vectors, positions):
    half_dim = DH // 2
    angles = positions[:, None].astype(jnp.float32) * frequencies()[None, :]
    cosine = jnp.cos(angles)
    sine = jnp.sin(angles)
    first_half = vectors[..., :half_dim]
    second_half = vectors[..., half_dim:]
    return jnp.concatenate(
        [first_half * cosine - second_half * sine, second_half * cosine + first_half * sine], -1
    )


def document_of(positions, block_doc):
    block_ids = positions // BLOCK
    table_ids = jnp.arange(block_doc.shape[0], dtype=jnp.int32)
    matches = block_ids[:, None] == table_ids[None, :]
    return jnp.sum(jnp.where(matches, block_doc[None, :], 0), axis=1)


def attend_tile(state_in, query_rows, query_pos, query_doc, key_rows, value_rows, key_pos, key_doc, valid):
    allowed = (key_pos[None, :] <= query_pos[:, None]) & (query_doc[:, None] == key_doc[None, :]) & valid
    scale = DH ** (-0.5)
    run_max, run_sum, run_out = state_in
    scores = (
        jnp.einsum("hqe,ke->hqk", query_rows, key_rows, preferred_element_type=jnp.float32) * scale
    )
    scores = jnp.where(allowed[None], scores, masked_low)
    new_max = jnp.maximum(run_max, jnp.max(scores, axis=-1))
    weights_f = jnp.where(allowed[None], jnp.exp(scores - new_max[..., None]), 0.0)
    rescale = jnp.exp(run_max - new_max)
    new_sum = run_sum * rescale + jnp.sum(weights_f, axis=-1)
    new_out = run_out * rescale[..., None] + jnp.einsum(
        "hqk,ke->hqe",
        weights_f.astype(jnp.bfloat16),
        value_rows,
        preferred_element_type=jnp.float32,
    )
    return (new_max, new_sum, new_out)


def flash_kernel(blocks_per_ctx, n_k, scalars, q_ref, k_ref, v_ref, o_ref, m_sc, l_sc, acc_sc):
    qi = pl.program_id(0)
    ki = pl.program_id(1)
    q_blk = scalars[0] * blocks_per_ctx + qi
    k_blk = scalars[1 + qi] + ki

    @pl.when(ki == 0)
    def _():
        m_sc[...] = jnp.full(m_sc.shape, masked_low, jnp.float32)
        l_sc[...] = jnp.zeros(l_sc.shape, jnp.float32)
        acc_sc[...] = jnp.zeros(acc_sc.shape, jnp.float32)

    def update(diagonal):
        scale = DH ** (-0.5)
        scores = lax.dot_general(
            q_ref[...], k_ref[...], (((1,), (1,)), ((), ())), preferred_element_type=jnp.float32
        ) * scale
        if diagonal:
            rows = lax.broadcasted_iota(jnp.int32, scores.shape, 0)
            cols = lax.broadcasted_iota(jnp.int32, scores.shape, 1)
            allowed = cols <= rows
            scores = jnp.where(allowed, scores, masked_low)
        m_prev = m_sc[...]
        m_new = jnp.maximum(m_prev, jnp.max(scores, axis=1, keepdims=True))
        weights = jnp.exp(scores - m_new[:, :1])
        if diagonal:
            weights = jnp.where(allowed, weights, 0.0)
        rescale = jnp.exp(m_prev - m_new)
        l_sc[...] = l_sc[...] * rescale + jnp.sum(weights, axis=1, keepdims=True)
        acc_sc[...] = acc_sc[...] * rescale + jnp.dot(
            weights.astype(jnp.bfloat16), v_ref[...], preferred_element_type=jnp.float32
        )
        m_sc[...] = m_new

    @pl.when(k_blk < q_blk)
    def _():
        update(False)

    @pl.when(k_blk == q_blk)
    def _():
        update(True)

    @pl.when(ki == n_k - 1)
    def _():
        o_ref[...] = (acc_sc[...] / l_sc[...]).astype(o_ref.dtype)


def flash_attend(me, block_doc, q_rot, kv_blocks):
    n_back, tok_rows, _ = kv_blocks.shape
    blocks_per_ctx = tok_rows // BLOCK
    n_q = blocks_per_ctx
    n_k = min(MAX_DOC_BLOCKS, n_back * blocks_per_ctx)
    q_blocks = me * blocks_per_ctx + jnp.arange(n_q, dtype=jnp.int32)
    first = jnp.sum(block_doc[None, :] < block_doc[q_blocks][:, None], axis=1).astype(jnp.int32)
    first = jnp.maximum(first, jnp.maximum(me - n_back + 1, 0) * blocks_per_ctx)
    scalars = jnp.concatenate([me.reshape(1).astype(jnp.int32), first])

    def kv_map(column):
        def index_map(qi, ki, sc):
            blk = jnp.minimum(sc[1 + qi] + ki, sc[0] * blocks_per_ctx + qi)
            return (sc[0] - blk // blocks_per_ctx, blk % blocks_per_ctx, column)

        return index_map

    grid_spec = pltpu.PrefetchScalarGridSpec(
        num_scalar_prefetch=1,
        grid=(n_q, n_k),
        in_specs=[
            pl.BlockSpec((BLOCK, DH), lambda qi, ki, sc: (qi, 0)),
            pl.BlockSpec((None, BLOCK, DH), kv_map(0)),
            pl.BlockSpec((None, BLOCK, DH), kv_map(1)),
        ],
        out_specs=pl.BlockSpec((BLOCK, DH), lambda qi, ki, sc: (qi, 0)),
        scratch_shapes=[
            pltpu.VMEM((BLOCK, DH), jnp.float32),
            pltpu.VMEM((BLOCK, DH), jnp.float32),
            pltpu.VMEM((BLOCK, DH), jnp.float32),
        ],
    )
    return pl.pallas_call(
        functools.partial(flash_kernel, blocks_per_ctx, n_k),
        out_shape=jax.ShapeDtypeStruct((tok_rows, DH), jnp.bfloat16),
        grid_spec=grid_spec,
        compiler_params=pltpu.CompilerParams(dimension_semantics=("arbitrary", "arbitrary")),
        cost_estimate=pl.CostEstimate(
            flops=4 * tok_rows * BLOCK * DH * n_k,
            transcendentals=tok_rows * BLOCK * n_k,
            bytes_accessed=2 * BLOCK * 2 * DH * n_k * n_q + 4 * tok_rows * DH,
        ),
    )(scalars, q_rot, kv_blocks, kv_blocks)


def gather_fsdp(piece, n_fsdp):
    me = lax.axis_index("fsdp")
    bits = n_fsdp.bit_length() - 1
    held = piece
    for bit in reversed(range(bits)):
        pairs = [(i, i ^ (1 << bit)) for i in range(n_fsdp)]
        theirs = lax.ppermute(held, "fsdp", pairs)
        mine_first = ((me >> bit) & 1) == 0
        held = jnp.where(mine_first, jnp.stack([held, theirs]), jnp.stack([theirs, held]))
    held = jnp.transpose(held, tuple(reversed(range(bits))) + tuple(range(bits, held.ndim)))
    return held.reshape((n_fsdp,) + piece.shape)


def on_device(hidden, w_query, w_key_value, block_doc):
    tok_rows, feat_rows = hidden.shape
    n_fsdp = lax.axis_size("fsdp")
    n_ctx = lax.axis_size("ctx")
    quarter = DH // 2 // n_fsdp
    eighth = DH // n_fsdp
    w_keys = w_key_value[:, :DH]
    w_comb = jnp.concatenate(
        [
            w_query.reshape(feat_rows, n_fsdp, DH),
            w_keys[:, : DH // 2].reshape(feat_rows, n_fsdp, quarter),
            w_keys[:, DH // 2 :].reshape(feat_rows, n_fsdp, quarter),
            w_key_value[:, DH:].reshape(feat_rows, n_fsdp, eighth),
        ],
        axis=2,
    )
    lanes = 128
    partial = jnp.einsum(
        "abd,dfc->fcab",
        hidden.reshape(tok_rows // lanes, lanes, feat_rows),
        w_comb,
        preferred_element_type=jnp.float32,
    )
    width = partial.shape[1]
    reduced = lax.psum_scatter(
        partial.reshape(n_fsdp, width * tok_rows // lanes, lanes), "fsdp", scatter_dimension=0, tiled=True
    ).reshape(width, tok_rows)
    me = lax.axis_index("ctx")
    me_f = lax.axis_index("fsdp")
    positions = me * tok_rows + jnp.arange(tok_rows, dtype=jnp.int32)
    half_dim = DH // 2
    angles = frequencies()[:, None] * positions[None, :].astype(jnp.float32)
    cosine = jnp.cos(angles)
    sine = jnp.sin(angles)
    q_a = reduced[:half_dim]
    q_b = reduced[half_dim:DH]
    q_rot = jnp.concatenate([q_a * cosine - q_b * sine, q_b * cosine + q_a * sine], 0)
    q_rot = jnp.transpose(q_rot.astype(jnp.bfloat16))
    key_a = reduced[DH : DH + quarter]
    key_b = reduced[DH + quarter : DH + 2 * quarter]
    vals = reduced[DH + 2 * quarter :]
    freq = lax.dynamic_slice_in_dim(frequencies(), me_f * quarter, quarter)
    k_angles = freq[:, None] * positions[None, :].astype(jnp.float32)
    k_cos = jnp.cos(k_angles)
    k_sin = jnp.sin(k_angles)
    piece = jnp.concatenate(
        [key_a * k_cos - key_b * k_sin, key_b * k_cos + key_a * k_sin, vals], axis=0
    ).astype(jnp.bfloat16)
    reach = min((MAX_DOC_BLOCKS * BLOCK - 1 + tok_rows - 1) // tok_rows, n_ctx - 1)
    pieces = jnp.stack(
        [piece]
        + [
            lax.ppermute(piece, "ctx", [(j, j + back) for j in range(n_ctx - back)])
            for back in range(1, reach + 1)
        ]
    )
    gathered = gather_fsdp(pieces, n_fsdp)

    def columns(lo, hi):
        part = jnp.transpose(gathered[:, :, lo:hi, :], (1, 3, 0, 2))
        return part.reshape(reach + 1, tok_rows, n_fsdp * (hi - lo))

    kv_blocks = jnp.concatenate(
        [columns(0, quarter), columns(quarter, 2 * quarter), columns(2 * quarter, 2 * quarter + eighth)],
        axis=2,
    )
    return flash_attend(me, block_doc, q_rot, kv_blocks)


def solution(mesh):
    return jax.shard_map(
        on_device,
        mesh=mesh,
        in_specs=(P("ctx", "fsdp"), P("fsdp", None), P("fsdp", None), P()),
        out_specs=P("ctx", "fsdp"),
        check_vma=False,
    )
```

```python
import functools

import jax
import jax.numpy as jnp
from jax import lax
from jax.experimental import pallas as pl
from jax.experimental.pallas import tpu as pltpu
from jax.sharding import PartitionSpec as P

DH = 128
HQ = 16
BLOCK = 512
MAX_DOC_BLOCKS = 16


masked_low = -1e30


def frequencies():
    half_dim = DH // 2
    return 500000.0 ** (-2.0 * jnp.arange(half_dim, dtype=jnp.float32) / DH)


def rotate_pairs(vectors, positions):
    half_dim = DH // 2
    angles = positions[:, None].astype(jnp.float32) * frequencies()[None, :]
    cosine = jnp.cos(angles)
    sine = jnp.sin(angles)
    first_half = vectors[..., :half_dim]
    second_half = vectors[..., half_dim:]
    return jnp.concatenate(
        [first_half * cosine - second_half * sine, second_half * cosine + first_half * sine], -1
    )


def document_of(positions, block_doc):
    block_ids = positions // BLOCK
    table_ids = jnp.arange(block_doc.shape[0], dtype=jnp.int32)
    matches = block_ids[:, None] == table_ids[None, :]
    return jnp.sum(jnp.where(matches, block_doc[None, :], 0), axis=1)


def attend_tile(state_in, query_rows, query_pos, query_doc, key_rows, value_rows, key_pos, key_doc, valid):
    allowed = (key_pos[None, :] <= query_pos[:, None]) & (query_doc[:, None] == key_doc[None, :]) & valid
    scale = DH ** (-0.5)
    run_max, run_sum, run_out = state_in
    scores = (
        jnp.einsum("hqe,ke->hqk", query_rows, key_rows, preferred_element_type=jnp.float32) * scale
    )
    scores = jnp.where(allowed[None], scores, masked_low)
    new_max = jnp.maximum(run_max, jnp.max(scores, axis=-1))
    weights_f = jnp.where(allowed[None], jnp.exp(scores - new_max[..., None]), 0.0)
    rescale = jnp.exp(run_max - new_max)
    new_sum = run_sum * rescale + jnp.sum(weights_f, axis=-1)
    new_out = run_out * rescale[..., None] + jnp.einsum(
        "hqk,ke->hqe",
        weights_f.astype(jnp.bfloat16),
        value_rows,
        preferred_element_type=jnp.float32,
    )
    return (new_max, new_sum, new_out)


def flash_kernel(blocks_per_ctx, n_k, scalars, q_ref, k_ref, v_ref, o_ref, m_sc, l_sc, acc_sc):
    qi = pl.program_id(0)
    ki = pl.program_id(1)
    q_blk = scalars[0] * blocks_per_ctx + qi
    k_blk = scalars[1 + qi] + ki

    @pl.when(ki == 0)
    def _():
        m_sc[...] = jnp.full(m_sc.shape, masked_low, jnp.float32)
        l_sc[...] = jnp.zeros(l_sc.shape, jnp.float32)
        acc_sc[...] = jnp.zeros(acc_sc.shape, jnp.float32)

    def update(diagonal):
        scale = DH ** (-0.5)
        scores = lax.dot_general(
            q_ref[...], k_ref[...], (((1,), (1,)), ((), ())), preferred_element_type=jnp.float32
        ) * scale
        if diagonal:
            rows = lax.broadcasted_iota(jnp.int32, scores.shape, 0)
            cols = lax.broadcasted_iota(jnp.int32, scores.shape, 1)
            allowed = cols <= rows
            scores = jnp.where(allowed, scores, masked_low)
        m_prev = m_sc[...]
        m_new = jnp.maximum(m_prev, jnp.max(scores, axis=1, keepdims=True))
        weights = jnp.exp(scores - m_new[:, :1])
        if diagonal:
            weights = jnp.where(allowed, weights, 0.0)
        rescale = jnp.exp(m_prev - m_new)
        l_sc[...] = l_sc[...] * rescale + jnp.sum(weights, axis=1, keepdims=True)
        acc_sc[...] = acc_sc[...] * rescale + jnp.dot(
            weights.astype(jnp.bfloat16), v_ref[...], preferred_element_type=jnp.float32
        )
        m_sc[...] = m_new

    @pl.when(k_blk < q_blk)
    def _():
        update(False)

    @pl.when(k_blk == q_blk)
    def _():
        update(True)

    @pl.when(ki == n_k - 1)
    def _():
        o_ref[...] = (acc_sc[...] / l_sc[...]).astype(o_ref.dtype)


def flash_attend(me, block_doc, q_rot, kv_blocks):
    n_back, tok_rows, _ = kv_blocks.shape
    blocks_per_ctx = tok_rows // BLOCK
    n_q = blocks_per_ctx
    n_k = min(MAX_DOC_BLOCKS, n_back * blocks_per_ctx)
    q_blocks = me * blocks_per_ctx + jnp.arange(n_q, dtype=jnp.int32)
    first = jnp.sum(block_doc[None, :] < block_doc[q_blocks][:, None], axis=1).astype(jnp.int32)
    first = jnp.maximum(first, jnp.maximum(me - n_back + 1, 0) * blocks_per_ctx)
    scalars = jnp.concatenate([me.reshape(1).astype(jnp.int32), first])

    def kv_map(column):
        def index_map(qi, ki, sc):
            blk = jnp.minimum(sc[1 + qi] + ki, sc[0] * blocks_per_ctx + qi)
            return (sc[0] - blk // blocks_per_ctx, blk % blocks_per_ctx, column)

        return index_map

    grid_spec = pltpu.PrefetchScalarGridSpec(
        num_scalar_prefetch=1,
        grid=(n_q, n_k),
        in_specs=[
            pl.BlockSpec((BLOCK, DH), lambda qi, ki, sc: (qi, 0)),
            pl.BlockSpec((None, BLOCK, DH), kv_map(0)),
            pl.BlockSpec((None, BLOCK, DH), kv_map(1)),
        ],
        out_specs=pl.BlockSpec((BLOCK, DH), lambda qi, ki, sc: (qi, 0)),
        scratch_shapes=[
            pltpu.VMEM((BLOCK, DH), jnp.float32),
            pltpu.VMEM((BLOCK, DH), jnp.float32),
            pltpu.VMEM((BLOCK, DH), jnp.float32),
        ],
    )
    return pl.pallas_call(
        functools.partial(flash_kernel, blocks_per_ctx, n_k),
        out_shape=jax.ShapeDtypeStruct((tok_rows, DH), jnp.bfloat16),
        grid_spec=grid_spec,
        compiler_params=pltpu.CompilerParams(dimension_semantics=("arbitrary", "arbitrary")),
        cost_estimate=pl.CostEstimate(
            flops=4 * tok_rows * BLOCK * DH * n_k,
            transcendentals=tok_rows * BLOCK * n_k,
            bytes_accessed=2 * BLOCK * 2 * DH * n_k * n_q + 4 * tok_rows * DH,
        ),
    )(scalars, q_rot, kv_blocks, kv_blocks)


def gather_fsdp(piece, n_fsdp):
    me = lax.axis_index("fsdp")
    bits = n_fsdp.bit_length() - 1
    held = piece
    for bit in reversed(range(bits)):
        pairs = [(i, i ^ (1 << bit)) for i in range(n_fsdp)]
        theirs = lax.ppermute(held, "fsdp", pairs)
        mine_first = ((me >> bit) & 1) == 0
        held = jnp.where(mine_first, jnp.stack([held, theirs]), jnp.stack([theirs, held]))
    held = jnp.transpose(held, tuple(reversed(range(bits))) + tuple(range(bits, held.ndim)))
    return held.reshape((n_fsdp,) + piece.shape)


def on_device(hidden, w_query, w_key_value, block_doc):
    tok_rows, feat_rows = hidden.shape
    n_fsdp = lax.axis_size("fsdp")
    n_ctx = lax.axis_size("ctx")
    quarter = DH // 2 // n_fsdp
    eighth = DH // n_fsdp
    lanes = 128
    hidden_rows = hidden.reshape(tok_rows // lanes, lanes, feat_rows)
    w_keys = w_key_value[:, :DH]
    w_kv = jnp.concatenate(
        [
            w_keys[:, : DH // 2].reshape(feat_rows, n_fsdp, quarter),
            w_keys[:, DH // 2 :].reshape(feat_rows, n_fsdp, quarter),
            w_key_value[:, DH:].reshape(feat_rows, n_fsdp, eighth),
        ],
        axis=2,
    )
    partial_kv = jnp.einsum("abd,dfc->fcab", hidden_rows, w_kv, preferred_element_type=jnp.float32)
    kv_width = partial_kv.shape[1]
    kv_sum = jnp.sum(lax.all_to_all(partial_kv, "fsdp", 0, 0, tiled=True), axis=0)
    kv_sum = kv_sum.reshape(kv_width, tok_rows)
    partial_q = jnp.einsum(
        "abd,dfc->fcab",
        hidden_rows,
        w_query.reshape(feat_rows, n_fsdp, DH),
        preferred_element_type=jnp.float32,
    )
    q_sum = lax.psum_scatter(
        partial_q.reshape(n_fsdp, DH * tok_rows // lanes, lanes), "fsdp", scatter_dimension=0, tiled=True
    ).reshape(DH, tok_rows)
    me = lax.axis_index("ctx")
    me_f = lax.axis_index("fsdp")
    positions = me * tok_rows + jnp.arange(tok_rows, dtype=jnp.int32)
    half_dim = DH // 2
    angles = frequencies()[:, None] * positions[None, :].astype(jnp.float32)
    cosine = jnp.cos(angles)
    sine = jnp.sin(angles)
    q_a = q_sum[:half_dim]
    q_b = q_sum[half_dim:]
    q_rot = jnp.concatenate([q_a * cosine - q_b * sine, q_b * cosine + q_a * sine], 0)
    q_rot = jnp.transpose(q_rot.astype(jnp.bfloat16))
    key_a = kv_sum[:quarter]
    key_b = kv_sum[quarter : 2 * quarter]
    vals = kv_sum[2 * quarter :]
    freq = lax.dynamic_slice_in_dim(frequencies(), me_f * quarter, quarter)
    k_angles = freq[:, None] * positions[None, :].astype(jnp.float32)
    k_cos = jnp.cos(k_angles)
    k_sin = jnp.sin(k_angles)
    piece = jnp.concatenate(
        [key_a * k_cos - key_b * k_sin, key_b * k_cos + key_a * k_sin, vals], axis=0
    ).astype(jnp.bfloat16)
    reach = min((MAX_DOC_BLOCKS * BLOCK - 1 + tok_rows - 1) // tok_rows, n_ctx - 1)
    pieces = jnp.stack(
        [piece]
        + [
            lax.ppermute(piece, "ctx", [(j, j + back) for j in range(n_ctx - back)])
            for back in range(1, reach + 1)
        ]
    )
    gathered = gather_fsdp(pieces, n_fsdp)

    def columns(lo, hi):
        part = jnp.transpose(gathered[:, :, lo:hi, :], (1, 3, 0, 2))
        return part.reshape(reach + 1, tok_rows, n_fsdp * (hi - lo))

    kv_blocks = jnp.concatenate(
        [columns(0, quarter), columns(quarter, 2 * quarter), columns(2 * quarter, 2 * quarter + eighth)],
        axis=2,
    )
    return flash_attend(me, block_doc, q_rot, kv_blocks)


def solution(mesh):
    return jax.shard_map(
        on_device,
        mesh=mesh,
        in_specs=(P("ctx", "fsdp"), P("fsdp", None), P("fsdp", None), P()),
        out_specs=P("ctx", "fsdp"),
        check_vma=False,
    )
```

```python
import functools

import jax
import jax.numpy as jnp
from jax import lax
from jax.experimental import pallas as pl
from jax.experimental.pallas import tpu as pltpu
from jax.sharding import PartitionSpec as P

DH = 128
HQ = 16
BLOCK = 512
MAX_DOC_BLOCKS = 16


masked_low = -1e30


def frequencies():
    half_dim = DH // 2
    return 500000.0 ** (-2.0 * jnp.arange(half_dim, dtype=jnp.float32) / DH)


def rotate_pairs(vectors, positions):
    half_dim = DH // 2
    angles = positions[:, None].astype(jnp.float32) * frequencies()[None, :]
    cosine = jnp.cos(angles)
    sine = jnp.sin(angles)
    first_half = vectors[..., :half_dim]
    second_half = vectors[..., half_dim:]
    return jnp.concatenate(
        [first_half * cosine - second_half * sine, second_half * cosine + first_half * sine], -1
    )


def document_of(positions, block_doc):
    block_ids = positions // BLOCK
    table_ids = jnp.arange(block_doc.shape[0], dtype=jnp.int32)
    matches = block_ids[:, None] == table_ids[None, :]
    return jnp.sum(jnp.where(matches, block_doc[None, :], 0), axis=1)


def attend_tile(state_in, query_rows, query_pos, query_doc, key_rows, value_rows, key_pos, key_doc, valid):
    allowed = (key_pos[None, :] <= query_pos[:, None]) & (query_doc[:, None] == key_doc[None, :]) & valid
    scale = DH ** (-0.5)
    run_max, run_sum, run_out = state_in
    scores = (
        jnp.einsum("hqe,ke->hqk", query_rows, key_rows, preferred_element_type=jnp.float32) * scale
    )
    scores = jnp.where(allowed[None], scores, masked_low)
    new_max = jnp.maximum(run_max, jnp.max(scores, axis=-1))
    weights_f = jnp.where(allowed[None], jnp.exp(scores - new_max[..., None]), 0.0)
    rescale = jnp.exp(run_max - new_max)
    new_sum = run_sum * rescale + jnp.sum(weights_f, axis=-1)
    new_out = run_out * rescale[..., None] + jnp.einsum(
        "hqk,ke->hqe",
        weights_f.astype(jnp.bfloat16),
        value_rows,
        preferred_element_type=jnp.float32,
    )
    return (new_max, new_sum, new_out)


def flash_kernel(blocks_per_ctx, n_k, scalars, q_ref, k_ref, v_ref, o_ref, m_sc, l_sc, acc_sc):
    qi = pl.program_id(0)
    ki = pl.program_id(1)
    q_blk = scalars[0] * blocks_per_ctx + qi
    k_blk = scalars[1 + qi] + ki

    @pl.when(ki == 0)
    def _():
        m_sc[...] = jnp.full(m_sc.shape, masked_low, jnp.float32)
        l_sc[...] = jnp.zeros(l_sc.shape, jnp.float32)
        acc_sc[...] = jnp.zeros(acc_sc.shape, jnp.float32)

    def update(diagonal):
        scale = DH ** (-0.5)
        scores = jnp.dot(q_ref[...], k_ref[...], preferred_element_type=jnp.float32) * scale
        if diagonal:
            rows = lax.broadcasted_iota(jnp.int32, scores.shape, 0)
            cols = lax.broadcasted_iota(jnp.int32, scores.shape, 1)
            allowed = cols <= rows
            scores = jnp.where(allowed, scores, masked_low)
        m_prev = m_sc[...]
        m_new = jnp.maximum(m_prev, jnp.max(scores, axis=1, keepdims=True))
        weights = jnp.exp(scores - m_new[:, :1])
        if diagonal:
            weights = jnp.where(allowed, weights, 0.0)
        rescale = jnp.exp(m_prev - m_new)
        l_sc[...] = l_sc[...] * rescale + jnp.sum(weights, axis=1, keepdims=True)
        acc_sc[...] = acc_sc[...] * rescale + jnp.dot(
            weights.astype(jnp.bfloat16), v_ref[...], preferred_element_type=jnp.float32
        )
        m_sc[...] = m_new

    @pl.when(k_blk < q_blk)
    def _():
        update(False)

    @pl.when(k_blk == q_blk)
    def _():
        update(True)

    @pl.when(ki == n_k - 1)
    def _():
        o_ref[...] = (acc_sc[...] / l_sc[...]).astype(o_ref.dtype)


def flash_attend(me, block_doc, q_rot, keys_t, values):
    n_back, _, tok_rows = keys_t.shape
    blocks_per_ctx = tok_rows // BLOCK
    n_q = blocks_per_ctx
    n_k = min(MAX_DOC_BLOCKS, n_back * blocks_per_ctx)
    q_blocks = me * blocks_per_ctx + jnp.arange(n_q, dtype=jnp.int32)
    first = jnp.sum(block_doc[None, :] < block_doc[q_blocks][:, None], axis=1).astype(jnp.int32)
    first = jnp.maximum(first, jnp.maximum(me - n_back + 1, 0) * blocks_per_ctx)
    scalars = jnp.concatenate([me.reshape(1).astype(jnp.int32), first])

    def key_block(qi, ki, sc):
        blk = jnp.minimum(sc[1 + qi] + ki, sc[0] * blocks_per_ctx + qi)
        return sc[0] - blk // blocks_per_ctx, blk % blocks_per_ctx

    grid_spec = pltpu.PrefetchScalarGridSpec(
        num_scalar_prefetch=1,
        grid=(n_q, n_k),
        in_specs=[
            pl.BlockSpec((BLOCK, DH), lambda qi, ki, sc: (qi, 0)),
            pl.BlockSpec((None, DH, BLOCK), lambda qi, ki, sc: (key_block(qi, ki, sc)[0], 0, key_block(qi, ki, sc)[1])),
            pl.BlockSpec((None, BLOCK, DH), lambda qi, ki, sc: key_block(qi, ki, sc) + (0,)),
        ],
        out_specs=pl.BlockSpec((BLOCK, DH), lambda qi, ki, sc: (qi, 0)),
        scratch_shapes=[
            pltpu.VMEM((BLOCK, DH), jnp.float32),
            pltpu.VMEM((BLOCK, DH), jnp.float32),
            pltpu.VMEM((BLOCK, DH), jnp.float32),
        ],
    )
    return pl.pallas_call(
        functools.partial(flash_kernel, blocks_per_ctx, n_k),
        out_shape=jax.ShapeDtypeStruct((tok_rows, DH), jnp.bfloat16),
        grid_spec=grid_spec,
        compiler_params=pltpu.CompilerParams(dimension_semantics=("arbitrary", "arbitrary")),
        cost_estimate=pl.CostEstimate(
            flops=4 * tok_rows * BLOCK * DH * n_k,
            transcendentals=tok_rows * BLOCK * n_k,
            bytes_accessed=2 * BLOCK * 2 * DH * n_k * n_q + 4 * tok_rows * DH,
        ),
    )(scalars, q_rot, keys_t, values)


def gather_fsdp(piece, n_fsdp):
    me = lax.axis_index("fsdp")
    bits = n_fsdp.bit_length() - 1
    held = piece
    for bit in reversed(range(bits)):
        pairs = [(i, i ^ (1 << bit)) for i in range(n_fsdp)]
        theirs = lax.ppermute(held, "fsdp", pairs)
        mine_first = ((me >> bit) & 1) == 0
        held = jnp.where(mine_first, jnp.stack([held, theirs]), jnp.stack([theirs, held]))
    held = jnp.transpose(held, tuple(reversed(range(bits))) + tuple(range(bits, held.ndim)))
    return held.reshape((n_fsdp,) + piece.shape)


def on_device(hidden, w_query, w_key_value, block_doc):
    tok_rows, feat_rows = hidden.shape
    n_fsdp = lax.axis_size("fsdp")
    n_ctx = lax.axis_size("ctx")
    half_dim = DH // 2
    lanes = 128
    key_devs = n_fsdp // 2
    pairs = half_dim // key_devs
    rows = 2 * pairs
    w_keys = w_key_value[:, :DH]
    w_kv = jnp.concatenate(
        [
            jnp.concatenate(
                [
                    w_keys[:, :half_dim].reshape(feat_rows, key_devs, pairs),
                    w_keys[:, half_dim:].reshape(feat_rows, key_devs, pairs),
                ],
                axis=2,
            ),
            w_key_value[:, DH:].reshape(feat_rows, n_fsdp - key_devs, rows),
        ],
        axis=1,
    )
    hidden_rows = hidden.reshape(tok_rows // lanes, lanes, feat_rows)
    partial_kv = jnp.einsum("abd,dfc->fcab", hidden_rows, w_kv, preferred_element_type=jnp.float32)
    kv_sum = jnp.sum(lax.all_to_all(partial_kv, "fsdp", 0, 0, tiled=True), axis=0)
    kv_sum = kv_sum.reshape(rows, tok_rows)
    partial_q = jnp.einsum(
        "abd,dfc->fcab",
        hidden_rows,
        w_query.reshape(feat_rows, n_fsdp, DH),
        preferred_element_type=jnp.float32,
    )
    q_sum = lax.psum_scatter(
        partial_q.reshape(n_fsdp, DH * tok_rows // lanes, lanes), "fsdp", scatter_dimension=0, tiled=True
    ).reshape(DH, tok_rows)
    me = lax.axis_index("ctx")
    me_f = lax.axis_index("fsdp")
    positions = me * tok_rows + jnp.arange(tok_rows, dtype=jnp.int32)
    angles = frequencies()[:, None] * positions[None, :].astype(jnp.float32)
    cosine = jnp.cos(angles)
    sine = jnp.sin(angles)
    q_a = q_sum[:half_dim]
    q_b = q_sum[half_dim:]
    q_rot = jnp.concatenate([q_a * cosine - q_b * sine, q_b * cosine + q_a * sine], 0).astype(jnp.bfloat16)
    q_rot = q_rot.reshape(2, key_devs, pairs, tok_rows).transpose(1, 0, 2, 3).reshape(DH, tok_rows)
    q_rot = jnp.transpose(q_rot)
    key_a = kv_sum[:pairs]
    key_b = kv_sum[pairs:]
    freq = lax.dynamic_slice_in_dim(frequencies(), (me_f % key_devs) * pairs, pairs)
    k_angles = freq[:, None] * positions[None, :].astype(jnp.float32)
    k_cos = jnp.cos(k_angles)
    k_sin = jnp.sin(k_angles)
    rotated = jnp.concatenate([key_a * k_cos - key_b * k_sin, key_b * k_cos + key_a * k_sin], axis=0)
    piece = jnp.where(me_f < key_devs, rotated, kv_sum).astype(jnp.bfloat16)
    reach = min((MAX_DOC_BLOCKS * BLOCK - 1 + tok_rows - 1) // tok_rows, n_ctx - 1)
    pieces = jnp.stack(
        [piece]
        + [
            lax.ppermute(piece, "ctx", [(j, j + back) for j in range(n_ctx - back)])
            for back in range(1, reach + 1)
        ]
    )
    gathered = jnp.transpose(gather_fsdp(pieces, n_fsdp), (1, 0, 2, 3))
    keys_t = gathered[:, :key_devs].reshape(reach + 1, DH, tok_rows)
    values = jnp.transpose(gathered[:, key_devs:].reshape(reach + 1, DH, tok_rows), (0, 2, 1))
    return flash_attend(me, block_doc, q_rot, keys_t, values)


def solution(mesh):
    return jax.shard_map(
        on_device,
        mesh=mesh,
        in_specs=(P("ctx", "fsdp"), P("fsdp", None), P("fsdp", None), P()),
        out_specs=P("ctx", "fsdp"),
        check_vma=False,
    )
```

```python
import functools

import jax
import jax.numpy as jnp
from jax import lax
from jax.experimental import pallas as pl
from jax.experimental.pallas import tpu as pltpu
from jax.sharding import PartitionSpec as P

DH = 128
HQ = 16
BLOCK = 512
MAX_DOC_BLOCKS = 16


masked_low = -1e30


def frequencies():
    half_dim = DH // 2
    return 500000.0 ** (-2.0 * jnp.arange(half_dim, dtype=jnp.float32) / DH)


def rotate_pairs(vectors, positions):
    half_dim = DH // 2
    angles = positions[:, None].astype(jnp.float32) * frequencies()[None, :]
    cosine = jnp.cos(angles)
    sine = jnp.sin(angles)
    first_half = vectors[..., :half_dim]
    second_half = vectors[..., half_dim:]
    return jnp.concatenate(
        [first_half * cosine - second_half * sine, second_half * cosine + first_half * sine], -1
    )


def document_of(positions, block_doc):
    block_ids = positions // BLOCK
    table_ids = jnp.arange(block_doc.shape[0], dtype=jnp.int32)
    matches = block_ids[:, None] == table_ids[None, :]
    return jnp.sum(jnp.where(matches, block_doc[None, :], 0), axis=1)


def attend_tile(state_in, query_rows, query_pos, query_doc, key_rows, value_rows, key_pos, key_doc, valid):
    allowed = (key_pos[None, :] <= query_pos[:, None]) & (query_doc[:, None] == key_doc[None, :]) & valid
    scale = DH ** (-0.5)
    run_max, run_sum, run_out = state_in
    scores = (
        jnp.einsum("hqe,ke->hqk", query_rows, key_rows, preferred_element_type=jnp.float32) * scale
    )
    scores = jnp.where(allowed[None], scores, masked_low)
    new_max = jnp.maximum(run_max, jnp.max(scores, axis=-1))
    weights_f = jnp.where(allowed[None], jnp.exp(scores - new_max[..., None]), 0.0)
    rescale = jnp.exp(run_max - new_max)
    new_sum = run_sum * rescale + jnp.sum(weights_f, axis=-1)
    new_out = run_out * rescale[..., None] + jnp.einsum(
        "hqk,ke->hqe",
        weights_f.astype(jnp.bfloat16),
        value_rows,
        preferred_element_type=jnp.float32,
    )
    return (new_max, new_sum, new_out)


def flash_kernel(blocks_per_ctx, n_k, scalars, q_ref, k_ref, v_ref, o_ref, m_sc, l_sc, acc_sc):
    ki = pl.program_id(0)
    k_blk = scalars[1] + ki

    @pl.when(ki == 0)
    def _():
        m_sc[...] = jnp.full(m_sc.shape, masked_low, jnp.float32)
        l_sc[...] = jnp.zeros(l_sc.shape, jnp.float32)
        acc_sc[...] = jnp.zeros(acc_sc.shape, jnp.float32)

    def update(rows, diagonal):
        scale = DH ** (-0.5)
        scores = jnp.dot(q_ref[rows, :], k_ref[...], preferred_element_type=jnp.float32) * scale
        if diagonal:
            row_ids = lax.broadcasted_iota(jnp.int32, scores.shape, 0)
            col_ids = lax.broadcasted_iota(jnp.int32, scores.shape, 1)
            allowed = col_ids <= row_ids
            scores = jnp.where(allowed, scores, masked_low)
        m_prev = m_sc[rows, :]
        m_new = jnp.maximum(m_prev, jnp.max(scores, axis=1, keepdims=True))
        weights = jnp.exp(scores - m_new[:, :1])
        if diagonal:
            weights = jnp.where(allowed, weights, 0.0)
        rescale = jnp.exp(m_prev - m_new)
        l_sc[rows, :] = l_sc[rows, :] * rescale + jnp.sum(weights, axis=1, keepdims=True)
        acc_sc[rows, :] = acc_sc[rows, :] * rescale + jnp.dot(
            weights.astype(jnp.bfloat16), v_ref[...], preferred_element_type=jnp.float32
        )
        m_sc[rows, :] = m_new

    for sub in range(blocks_per_ctx):
        q_blk = scalars[0] * blocks_per_ctx + sub
        rows = pl.ds(sub * BLOCK, BLOCK)

        @pl.when((k_blk >= scalars[1 + sub]) & (k_blk < q_blk))
        def _():
            update(rows, False)

        @pl.when(k_blk == q_blk)
        def _():
            update(rows, True)

    @pl.when(ki == n_k - 1)
    def _():
        o_ref[...] = (acc_sc[...] / l_sc[...]).astype(o_ref.dtype)


def flash_attend(me, block_doc, q_rot, keys_t, values):
    n_back, _, tok_rows = keys_t.shape
    blocks_per_ctx = tok_rows // BLOCK
    n_k = min(MAX_DOC_BLOCKS + blocks_per_ctx - 1, n_back * blocks_per_ctx)
    q_blocks = me * blocks_per_ctx + jnp.arange(blocks_per_ctx, dtype=jnp.int32)
    first = jnp.sum(block_doc[None, :] < block_doc[q_blocks][:, None], axis=1).astype(jnp.int32)
    first = jnp.maximum(first, jnp.maximum(me - n_back + 1, 0) * blocks_per_ctx)
    scalars = jnp.concatenate([me.reshape(1).astype(jnp.int32), first])

    def key_block(ki, sc):
        blk = jnp.minimum(sc[1] + ki, sc[0] * blocks_per_ctx + blocks_per_ctx - 1)
        return sc[0] - blk // blocks_per_ctx, blk % blocks_per_ctx

    grid_spec = pltpu.PrefetchScalarGridSpec(
        num_scalar_prefetch=1,
        grid=(n_k,),
        in_specs=[
            pl.BlockSpec((tok_rows, DH), lambda ki, sc: (0, 0)),
            pl.BlockSpec((None, DH, BLOCK), lambda ki, sc: (key_block(ki, sc)[0], 0, key_block(ki, sc)[1])),
            pl.BlockSpec((None, BLOCK, DH), lambda ki, sc: key_block(ki, sc) + (0,)),
        ],
        out_specs=pl.BlockSpec((tok_rows, DH), lambda ki, sc: (0, 0)),
        scratch_shapes=[
            pltpu.VMEM((tok_rows, DH), jnp.float32),
            pltpu.VMEM((tok_rows, DH), jnp.float32),
            pltpu.VMEM((tok_rows, DH), jnp.float32),
        ],
    )
    return pl.pallas_call(
        functools.partial(flash_kernel, blocks_per_ctx, n_k),
        out_shape=jax.ShapeDtypeStruct((tok_rows, DH), jnp.bfloat16),
        grid_spec=grid_spec,
        compiler_params=pltpu.CompilerParams(dimension_semantics=("arbitrary",)),
        cost_estimate=pl.CostEstimate(
            flops=4 * BLOCK * BLOCK * DH * MAX_DOC_BLOCKS * blocks_per_ctx,
            transcendentals=BLOCK * BLOCK * MAX_DOC_BLOCKS * blocks_per_ctx,
            bytes_accessed=2 * BLOCK * 2 * DH * n_k + 4 * tok_rows * DH,
        ),
    )(scalars, q_rot, keys_t, values)


def gather_fsdp(piece, n_fsdp):
    me = lax.axis_index("fsdp")
    bits = n_fsdp.bit_length() - 1
    held = piece
    for bit in reversed(range(bits)):
        pairs = [(i, i ^ (1 << bit)) for i in range(n_fsdp)]
        theirs = lax.ppermute(held, "fsdp", pairs)
        mine_first = ((me >> bit) & 1) == 0
        held = jnp.where(mine_first, jnp.stack([held, theirs]), jnp.stack([theirs, held]))
    held = jnp.transpose(held, tuple(reversed(range(bits))) + tuple(range(bits, held.ndim)))
    return held.reshape((n_fsdp,) + piece.shape)


def on_device(hidden, w_query, w_key_value, block_doc):
    tok_rows, feat_rows = hidden.shape
    n_fsdp = lax.axis_size("fsdp")
    n_ctx = lax.axis_size("ctx")
    half_dim = DH // 2
    lanes = 128
    key_devs = n_fsdp // 2
    pairs = half_dim // key_devs
    rows = 2 * pairs
    w_keys = w_key_value[:, :DH]
    w_kv = jnp.concatenate(
        [
            jnp.concatenate(
                [
                    w_keys[:, :half_dim].reshape(feat_rows, key_devs, pairs),
                    w_keys[:, half_dim:].reshape(feat_rows, key_devs, pairs),
                ],
                axis=2,
            ),
            w_key_value[:, DH:].reshape(feat_rows, n_fsdp - key_devs, rows),
        ],
        axis=1,
    )
    hidden_rows = hidden.reshape(tok_rows // lanes, lanes, feat_rows)
    partial_kv = jnp.einsum("abd,dfc->fcab", hidden_rows, w_kv, preferred_element_type=jnp.float32)
    kv_sum = jnp.sum(lax.all_to_all(partial_kv, "fsdp", 0, 0, tiled=True), axis=0)
    kv_sum = kv_sum.reshape(rows, tok_rows)
    q_sum = lax.psum_scatter(
        jnp.einsum("td,dfc->ftc", hidden, w_query.reshape(feat_rows, n_fsdp, DH), preferred_element_type=jnp.float32),
        "fsdp",
        scatter_dimension=0,
        tiled=True,
    )[0]
    me = lax.axis_index("ctx")
    me_f = lax.axis_index("fsdp")
    positions = me * tok_rows + jnp.arange(tok_rows, dtype=jnp.int32)
    q_rot = rotate_pairs(q_sum, positions).astype(jnp.bfloat16)
    q_rot = q_rot.reshape(tok_rows, 2, key_devs, pairs).transpose(0, 2, 1, 3).reshape(tok_rows, DH)
    key_a = kv_sum[:pairs]
    key_b = kv_sum[pairs:]
    freq = lax.dynamic_slice_in_dim(frequencies(), (me_f % key_devs) * pairs, pairs)
    k_angles = freq[:, None] * positions[None, :].astype(jnp.float32)
    k_cos = jnp.cos(k_angles)
    k_sin = jnp.sin(k_angles)
    rotated = jnp.concatenate([key_a * k_cos - key_b * k_sin, key_b * k_cos + key_a * k_sin], axis=0)
    piece = jnp.where(me_f < key_devs, rotated, kv_sum).astype(jnp.bfloat16)
    reach = min((MAX_DOC_BLOCKS * BLOCK - 1 + tok_rows - 1) // tok_rows, n_ctx - 1)
    pieces = jnp.stack(
        [piece]
        + [
            lax.ppermute(piece, "ctx", [(j, j + back) for j in range(n_ctx - back)])
            for back in range(1, reach + 1)
        ]
    )
    gathered = jnp.transpose(gather_fsdp(pieces, n_fsdp), (1, 0, 2, 3))
    keys_t = gathered[:, :key_devs].reshape(reach + 1, DH, tok_rows)
    values = jnp.transpose(gathered[:, key_devs:].reshape(reach + 1, DH, tok_rows), (0, 2, 1))
    return flash_attend(me, block_doc, q_rot, keys_t, values)


def solution(mesh):
    return jax.shard_map(
        on_device,
        mesh=mesh,
        in_specs=(P("ctx", "fsdp"), P("fsdp", None), P("fsdp", None), P()),
        out_specs=P("ctx", "fsdp"),
        check_vma=False,
    )
```

```python
import functools

import jax
import jax.numpy as jnp
from jax import lax
from jax.experimental import pallas as pl
from jax.experimental.pallas import tpu as pltpu
from jax.sharding import PartitionSpec as P

DH = 128
HQ = 16
BLOCK = 512
MAX_DOC_BLOCKS = 16


masked_low = -1e30


def frequencies():
    half_dim = DH // 2
    return 500000.0 ** (-2.0 * jnp.arange(half_dim, dtype=jnp.float32) / DH)


def rotate_pairs(vectors, positions):
    half_dim = DH // 2
    angles = positions[:, None].astype(jnp.float32) * frequencies()[None, :]
    cosine = jnp.cos(angles)
    sine = jnp.sin(angles)
    first_half = vectors[..., :half_dim]
    second_half = vectors[..., half_dim:]
    return jnp.concatenate(
        [first_half * cosine - second_half * sine, second_half * cosine + first_half * sine], -1
    )


def document_of(positions, block_doc):
    block_ids = positions // BLOCK
    table_ids = jnp.arange(block_doc.shape[0], dtype=jnp.int32)
    matches = block_ids[:, None] == table_ids[None, :]
    return jnp.sum(jnp.where(matches, block_doc[None, :], 0), axis=1)


def attend_tile(state_in, query_rows, query_pos, query_doc, key_rows, value_rows, key_pos, key_doc, valid):
    allowed = (key_pos[None, :] <= query_pos[:, None]) & (query_doc[:, None] == key_doc[None, :]) & valid
    scale = DH ** (-0.5)
    run_max, run_sum, run_out = state_in
    scores = (
        jnp.einsum("hqe,ke->hqk", query_rows, key_rows, preferred_element_type=jnp.float32) * scale
    )
    scores = jnp.where(allowed[None], scores, masked_low)
    new_max = jnp.maximum(run_max, jnp.max(scores, axis=-1))
    weights_f = jnp.where(allowed[None], jnp.exp(scores - new_max[..., None]), 0.0)
    rescale = jnp.exp(run_max - new_max)
    new_sum = run_sum * rescale + jnp.sum(weights_f, axis=-1)
    new_out = run_out * rescale[..., None] + jnp.einsum(
        "hqk,ke->hqe",
        weights_f.astype(jnp.bfloat16),
        value_rows,
        preferred_element_type=jnp.float32,
    )
    return (new_max, new_sum, new_out)


def flash_kernel(blocks_per_ctx, n_k, scalars, q_ref, k_ref, v_ref, o_ref, m_sc, l_sc, acc_sc):
    ki = pl.program_id(0)
    k_blk = scalars[1] + ki

    @pl.when(ki == 0)
    def _():
        m_sc[...] = jnp.full(m_sc.shape, masked_low, jnp.float32)
        l_sc[...] = jnp.zeros(l_sc.shape, jnp.float32)
        acc_sc[...] = jnp.zeros(acc_sc.shape, jnp.float32)

    def update(rows, diagonal):
        scale = DH ** (-0.5)
        scores = jnp.dot(q_ref[rows, :], k_ref[...], preferred_element_type=jnp.float32) * scale
        if diagonal:
            row_ids = lax.broadcasted_iota(jnp.int32, scores.shape, 0)
            col_ids = lax.broadcasted_iota(jnp.int32, scores.shape, 1)
            allowed = col_ids <= row_ids
            scores = jnp.where(allowed, scores, masked_low)
        m_prev = m_sc[rows, :]
        m_new = jnp.maximum(m_prev, jnp.max(scores, axis=1, keepdims=True))
        weights = jnp.exp(scores - m_new[:, :1])
        if diagonal:
            weights = jnp.where(allowed, weights, 0.0)
        rescale = jnp.exp(m_prev - m_new)
        l_sc[rows, :] = l_sc[rows, :] * rescale + jnp.sum(weights, axis=1, keepdims=True)
        acc_sc[rows, :] = acc_sc[rows, :] * rescale + jnp.dot(
            weights.astype(jnp.bfloat16), v_ref[...], preferred_element_type=jnp.float32
        )
        m_sc[rows, :] = m_new

    interior = (k_blk >= scalars[blocks_per_ctx]) & (k_blk < scalars[0] * blocks_per_ctx)

    @pl.when(interior)
    def _():
        update(pl.ds(0, blocks_per_ctx * BLOCK), False)

    for sub in range(blocks_per_ctx):
        q_blk = scalars[0] * blocks_per_ctx + sub
        rows = pl.ds(sub * BLOCK, BLOCK)

        @pl.when(jnp.logical_not(interior) & (k_blk >= scalars[1 + sub]) & (k_blk < q_blk))
        def _():
            update(rows, False)

        @pl.when(k_blk == q_blk)
        def _():
            update(rows, True)

    @pl.when(ki == n_k - 1)
    def _():
        o_ref[...] = (acc_sc[...] / l_sc[...]).astype(o_ref.dtype)


def flash_attend(me, block_doc, q_rot, keys_t, values):
    n_back, _, tok_rows = keys_t.shape
    blocks_per_ctx = tok_rows // BLOCK
    n_k = min(MAX_DOC_BLOCKS + blocks_per_ctx - 1, n_back * blocks_per_ctx)
    q_blocks = me * blocks_per_ctx + jnp.arange(blocks_per_ctx, dtype=jnp.int32)
    first = jnp.sum(block_doc[None, :] < block_doc[q_blocks][:, None], axis=1).astype(jnp.int32)
    first = jnp.maximum(first, jnp.maximum(me - n_back + 1, 0) * blocks_per_ctx)
    scalars = jnp.concatenate([me.reshape(1).astype(jnp.int32), first])

    def key_block(ki, sc):
        blk = jnp.minimum(sc[1] + ki, sc[0] * blocks_per_ctx + blocks_per_ctx - 1)
        return sc[0] - blk // blocks_per_ctx, blk % blocks_per_ctx

    grid_spec = pltpu.PrefetchScalarGridSpec(
        num_scalar_prefetch=1,
        grid=(n_k,),
        in_specs=[
            pl.BlockSpec((tok_rows, DH), lambda ki, sc: (0, 0)),
            pl.BlockSpec((None, DH, BLOCK), lambda ki, sc: (key_block(ki, sc)[0], 0, key_block(ki, sc)[1])),
            pl.BlockSpec((None, BLOCK, DH), lambda ki, sc: key_block(ki, sc) + (0,)),
        ],
        out_specs=pl.BlockSpec((tok_rows, DH), lambda ki, sc: (0, 0)),
        scratch_shapes=[
            pltpu.VMEM((tok_rows, DH), jnp.float32),
            pltpu.VMEM((tok_rows, DH), jnp.float32),
            pltpu.VMEM((tok_rows, DH), jnp.float32),
        ],
    )
    return pl.pallas_call(
        functools.partial(flash_kernel, blocks_per_ctx, n_k),
        out_shape=jax.ShapeDtypeStruct((tok_rows, DH), jnp.bfloat16),
        grid_spec=grid_spec,
        compiler_params=pltpu.CompilerParams(dimension_semantics=("arbitrary",)),
        cost_estimate=pl.CostEstimate(
            flops=4 * BLOCK * BLOCK * DH * MAX_DOC_BLOCKS * blocks_per_ctx,
            transcendentals=BLOCK * BLOCK * MAX_DOC_BLOCKS * blocks_per_ctx,
            bytes_accessed=2 * BLOCK * 2 * DH * n_k + 4 * tok_rows * DH,
        ),
    )(scalars, q_rot, keys_t, values)


def gather_fsdp(piece, n_fsdp):
    me = lax.axis_index("fsdp")
    bits = n_fsdp.bit_length() - 1
    held = piece
    for bit in reversed(range(bits)):
        pairs = [(i, i ^ (1 << bit)) for i in range(n_fsdp)]
        theirs = lax.ppermute(held, "fsdp", pairs)
        mine_first = ((me >> bit) & 1) == 0
        held = jnp.where(mine_first, jnp.stack([held, theirs]), jnp.stack([theirs, held]))
    held = jnp.transpose(held, tuple(reversed(range(bits))) + tuple(range(bits, held.ndim)))
    return held.reshape((n_fsdp,) + piece.shape)


def on_device(hidden, w_query, w_key_value, block_doc):
    tok_rows, feat_rows = hidden.shape
    n_fsdp = lax.axis_size("fsdp")
    n_ctx = lax.axis_size("ctx")
    half_dim = DH // 2
    lanes = 128
    key_devs = n_fsdp // 2
    pairs = half_dim // key_devs
    rows = 2 * pairs
    w_keys = w_key_value[:, :DH]
    w_kv = jnp.concatenate(
        [
            jnp.concatenate(
                [
                    w_keys[:, :half_dim].reshape(feat_rows, key_devs, pairs),
                    w_keys[:, half_dim:].reshape(feat_rows, key_devs, pairs),
                ],
                axis=2,
            ),
            w_key_value[:, DH:].reshape(feat_rows, n_fsdp - key_devs, rows),
        ],
        axis=1,
    )
    hidden_rows = hidden.reshape(tok_rows // lanes, lanes, feat_rows)
    partial_kv = jnp.einsum("abd,dfc->fcab", hidden_rows, w_kv, preferred_element_type=jnp.float32)
    kv_sum = jnp.sum(lax.all_to_all(partial_kv, "fsdp", 0, 0, tiled=True), axis=0)
    kv_sum = kv_sum.reshape(rows, tok_rows)
    q_sum = lax.psum_scatter(
        jnp.einsum("td,dfc->ftc", hidden, w_query.reshape(feat_rows, n_fsdp, DH), preferred_element_type=jnp.float32),
        "fsdp",
        scatter_dimension=0,
        tiled=True,
    )[0]
    me = lax.axis_index("ctx")
    me_f = lax.axis_index("fsdp")
    positions = me * tok_rows + jnp.arange(tok_rows, dtype=jnp.int32)
    q_rot = rotate_pairs(q_sum, positions).astype(jnp.bfloat16)
    q_rot = q_rot.reshape(tok_rows, 2, key_devs, pairs).transpose(0, 2, 1, 3).reshape(tok_rows, DH)
    key_a = kv_sum[:pairs]
    key_b = kv_sum[pairs:]
    freq = lax.dynamic_slice_in_dim(frequencies(), (me_f % key_devs) * pairs, pairs)
    k_angles = freq[:, None] * positions[None, :].astype(jnp.float32)
    k_cos = jnp.cos(k_angles)
    k_sin = jnp.sin(k_angles)
    rotated = jnp.concatenate([key_a * k_cos - key_b * k_sin, key_b * k_cos + key_a * k_sin], axis=0)
    piece = jnp.where(me_f < key_devs, rotated, kv_sum).astype(jnp.bfloat16)
    reach = min((MAX_DOC_BLOCKS * BLOCK - 1 + tok_rows - 1) // tok_rows, n_ctx - 1)
    pieces = jnp.stack(
        [piece]
        + [
            lax.ppermute(piece, "ctx", [(j, j + back) for j in range(n_ctx - back)])
            for back in range(1, reach + 1)
        ]
    )
    gathered = jnp.transpose(gather_fsdp(pieces, n_fsdp), (1, 0, 2, 3))
    keys_t = gathered[:, :key_devs].reshape(reach + 1, DH, tok_rows)
    values = jnp.transpose(gathered[:, key_devs:].reshape(reach + 1, DH, tok_rows), (0, 2, 1))
    return flash_attend(me, block_doc, q_rot, keys_t, values)


def solution(mesh):
    return jax.shard_map(
        on_device,
        mesh=mesh,
        in_specs=(P("ctx", "fsdp"), P("fsdp", None), P("fsdp", None), P()),
        out_specs=P("ctx", "fsdp"),
        check_vma=False,
    )
```

```python
import functools

import jax
import jax.numpy as jnp
from jax import lax
from jax.experimental import pallas as pl
from jax.experimental.pallas import tpu as pltpu
from jax.sharding import PartitionSpec as P

DH = 128
HQ = 16
BLOCK = 512
MAX_DOC_BLOCKS = 16
SUB_ROWS = 512


masked_low = -1e30


def frequencies():
    half_dim = DH // 2
    return 500000.0 ** (-2.0 * jnp.arange(half_dim, dtype=jnp.float32) / DH)


def rotate_pairs(vectors, positions):
    half_dim = DH // 2
    angles = positions[:, None].astype(jnp.float32) * frequencies()[None, :]
    cosine = jnp.cos(angles)
    sine = jnp.sin(angles)
    first_half = vectors[..., :half_dim]
    second_half = vectors[..., half_dim:]
    return jnp.concatenate(
        [first_half * cosine - second_half * sine, second_half * cosine + first_half * sine], -1
    )


def document_of(positions, block_doc):
    block_ids = positions // BLOCK
    table_ids = jnp.arange(block_doc.shape[0], dtype=jnp.int32)
    matches = block_ids[:, None] == table_ids[None, :]
    return jnp.sum(jnp.where(matches, block_doc[None, :], 0), axis=1)


def attend_tile(state_in, query_rows, query_pos, query_doc, key_rows, value_rows, key_pos, key_doc, valid):
    allowed = (key_pos[None, :] <= query_pos[:, None]) & (query_doc[:, None] == key_doc[None, :]) & valid
    scale = DH ** (-0.5)
    run_max, run_sum, run_out = state_in
    scores = (
        jnp.einsum("hqe,ke->hqk", query_rows, key_rows, preferred_element_type=jnp.float32) * scale
    )
    scores = jnp.where(allowed[None], scores, masked_low)
    new_max = jnp.maximum(run_max, jnp.max(scores, axis=-1))
    weights_f = jnp.where(allowed[None], jnp.exp(scores - new_max[..., None]), 0.0)
    rescale = jnp.exp(run_max - new_max)
    new_sum = run_sum * rescale + jnp.sum(weights_f, axis=-1)
    new_out = run_out * rescale[..., None] + jnp.einsum(
        "hqk,ke->hqe",
        weights_f.astype(jnp.bfloat16),
        value_rows,
        preferred_element_type=jnp.float32,
    )
    return (new_max, new_sum, new_out)


def flash_kernel(blocks_per_ctx, n_k, sub_rows, scalars, q_ref, k_ref, v_ref, o_ref, m_sc, l_sc, acc_sc):
    ki = pl.program_id(0)
    k_blk = scalars[1] + ki

    @pl.when(ki == 0)
    def _():
        m_sc[...] = jnp.full(m_sc.shape, masked_low, jnp.float32)
        l_sc[...] = jnp.zeros(l_sc.shape, jnp.float32)
        acc_sc[...] = jnp.zeros(acc_sc.shape, jnp.float32)

    def update(rows, offset):
        scale = DH ** (-0.5)
        scores = jnp.dot(q_ref[rows, :], k_ref[...], preferred_element_type=jnp.float32) * scale
        diagonal = offset is not None
        if diagonal:
            row_ids = lax.broadcasted_iota(jnp.int32, scores.shape, 0) + offset
            col_ids = lax.broadcasted_iota(jnp.int32, scores.shape, 1)
            allowed = col_ids <= row_ids
            scores = jnp.where(allowed, scores, masked_low)
        m_prev = m_sc[rows, :]
        m_new = jnp.maximum(m_prev, jnp.max(scores, axis=1, keepdims=True))
        weights = jnp.exp(scores - m_new[:, :1])
        if diagonal:
            weights = jnp.where(allowed, weights, 0.0)
        rescale = jnp.exp(m_prev - m_new)
        l_sc[rows, :] = l_sc[rows, :] * rescale + jnp.sum(weights, axis=1, keepdims=True)
        acc_sc[rows, :] = acc_sc[rows, :] * rescale + jnp.dot(
            weights.astype(jnp.bfloat16), v_ref[...], preferred_element_type=jnp.float32
        )
        m_sc[rows, :] = m_new

    for sub in range(blocks_per_ctx * BLOCK // sub_rows):
        q_sub = sub * sub_rows // BLOCK
        q_blk = scalars[0] * blocks_per_ctx + q_sub
        rows = pl.ds(sub * sub_rows, sub_rows)

        @pl.when((k_blk >= scalars[1 + q_sub]) & (k_blk < q_blk))
        def _():
            update(rows, None)

        @pl.when(k_blk == q_blk)
        def _():
            update(rows, sub * sub_rows % BLOCK)

    @pl.when(ki == n_k - 1)
    def _():
        o_ref[...] = (acc_sc[...] / l_sc[...]).astype(o_ref.dtype)


def flash_attend(me, block_doc, q_rot, keys_t, values, sub_rows=SUB_ROWS, flags=None):
    n_back, _, tok_rows = keys_t.shape
    blocks_per_ctx = tok_rows // BLOCK
    n_k = min(MAX_DOC_BLOCKS + blocks_per_ctx - 1, n_back * blocks_per_ctx)
    q_blocks = me * blocks_per_ctx + jnp.arange(blocks_per_ctx, dtype=jnp.int32)
    first = jnp.sum(block_doc[None, :] < block_doc[q_blocks][:, None], axis=1).astype(jnp.int32)
    first = jnp.maximum(first, jnp.maximum(me - n_back + 1, 0) * blocks_per_ctx)
    scalars = jnp.concatenate([me.reshape(1).astype(jnp.int32), first])

    def key_block(ki, sc):
        blk = jnp.minimum(sc[1] + ki, sc[0] * blocks_per_ctx + blocks_per_ctx - 1)
        return sc[0] - blk // blocks_per_ctx, blk % blocks_per_ctx

    grid_spec = pltpu.PrefetchScalarGridSpec(
        num_scalar_prefetch=1,
        grid=(n_k,),
        in_specs=[
            pl.BlockSpec((tok_rows, DH), lambda ki, sc: (0, 0)),
            pl.BlockSpec((None, DH, BLOCK), lambda ki, sc: (key_block(ki, sc)[0], 0, key_block(ki, sc)[1])),
            pl.BlockSpec((None, BLOCK, DH), lambda ki, sc: key_block(ki, sc) + (0,)),
        ],
        out_specs=pl.BlockSpec((tok_rows, DH), lambda ki, sc: (0, 0)),
        scratch_shapes=[
            pltpu.VMEM((tok_rows, DH), jnp.float32),
            pltpu.VMEM((tok_rows, DH), jnp.float32),
            pltpu.VMEM((tok_rows, DH), jnp.float32),
        ],
    )
    return pl.pallas_call(
        functools.partial(flash_kernel, blocks_per_ctx, n_k, sub_rows),
        out_shape=jax.ShapeDtypeStruct((tok_rows, DH), jnp.bfloat16),
        grid_spec=grid_spec,
        compiler_params=pltpu.CompilerParams(dimension_semantics=("arbitrary",), flags=flags),
        cost_estimate=pl.CostEstimate(
            flops=4 * BLOCK * BLOCK * DH * MAX_DOC_BLOCKS * blocks_per_ctx,
            transcendentals=BLOCK * BLOCK * MAX_DOC_BLOCKS * blocks_per_ctx,
            bytes_accessed=2 * BLOCK * 2 * DH * n_k + 4 * tok_rows * DH,
        ),
    )(scalars, q_rot, keys_t, values)


def gather_fsdp(piece, n_fsdp):
    me = lax.axis_index("fsdp")
    bits = n_fsdp.bit_length() - 1
    held = piece
    for bit in reversed(range(bits)):
        pairs = [(i, i ^ (1 << bit)) for i in range(n_fsdp)]
        theirs = lax.ppermute(held, "fsdp", pairs)
        mine_first = ((me >> bit) & 1) == 0
        held = jnp.where(mine_first, jnp.stack([held, theirs]), jnp.stack([theirs, held]))
    held = jnp.transpose(held, tuple(reversed(range(bits))) + tuple(range(bits, held.ndim)))
    return held.reshape((n_fsdp,) + piece.shape)


def on_device(hidden, w_query, w_key_value, block_doc):
    tok_rows, feat_rows = hidden.shape
    n_fsdp = lax.axis_size("fsdp")
    n_ctx = lax.axis_size("ctx")
    half_dim = DH // 2
    lanes = 128
    key_devs = n_fsdp // 2
    pairs = half_dim // key_devs
    rows = 2 * pairs
    w_keys = w_key_value[:, :DH]
    w_kv = jnp.concatenate(
        [
            jnp.concatenate(
                [
                    w_keys[:, :half_dim].reshape(feat_rows, key_devs, pairs),
                    w_keys[:, half_dim:].reshape(feat_rows, key_devs, pairs),
                ],
                axis=2,
            ),
            w_key_value[:, DH:].reshape(feat_rows, n_fsdp - key_devs, rows),
        ],
        axis=1,
    )
    hidden_rows = hidden.reshape(tok_rows // lanes, lanes, feat_rows)
    partial_kv = jnp.einsum("abd,dfc->fcab", hidden_rows, w_kv, preferred_element_type=jnp.float32)
    kv_sum = jnp.sum(lax.all_to_all(partial_kv, "fsdp", 0, 0, tiled=True), axis=0)
    kv_sum = kv_sum.reshape(rows, tok_rows)
    core = lax.axis_index("fsdp") % 2
    w_heads = w_query.reshape(feat_rows, n_fsdp // 2, 2, DH)
    w_other = jnp.where(core == 0, w_heads[:, :, 1], w_heads[:, :, 0])
    w_mine = jnp.where(core == 0, w_heads[:, :, 0], w_heads[:, :, 1])
    q_other = jnp.einsum("td,dfc->ftc", hidden, w_other, preferred_element_type=jnp.float32)
    q_got = lax.ppermute(q_other, "fsdp", [(i, i ^ 1) for i in range(n_fsdp)])
    q_mine = jnp.einsum("td,dfc->ftc", hidden, w_mine, preferred_element_type=jnp.float32)
    same_core = [[f for f in range(n_fsdp) if f % 2 == c] for c in range(2)]
    q_sum = lax.psum_scatter(
        q_mine + q_got, "fsdp", scatter_dimension=0, tiled=True, axis_index_groups=same_core
    )[0]
    me = lax.axis_index("ctx")
    me_f = lax.axis_index("fsdp")
    positions = me * tok_rows + jnp.arange(tok_rows, dtype=jnp.int32)
    q_rot = rotate_pairs(q_sum, positions).astype(jnp.bfloat16)
    q_rot = q_rot.reshape(tok_rows, 2, key_devs, pairs).transpose(0, 2, 1, 3).reshape(tok_rows, DH)
    key_a = kv_sum[:pairs]
    key_b = kv_sum[pairs:]
    freq = lax.dynamic_slice_in_dim(frequencies(), (me_f % key_devs) * pairs, pairs)
    k_angles = freq[:, None] * positions[None, :].astype(jnp.float32)
    k_cos = jnp.cos(k_angles)
    k_sin = jnp.sin(k_angles)
    rotated = jnp.concatenate([key_a * k_cos - key_b * k_sin, key_b * k_cos + key_a * k_sin], axis=0)
    piece = jnp.where(me_f < key_devs, rotated, kv_sum).astype(jnp.bfloat16)
    reach = min((MAX_DOC_BLOCKS * BLOCK - 1 + tok_rows - 1) // tok_rows, n_ctx - 1)
    pieces = jnp.stack(
        [piece]
        + [
            lax.ppermute(piece, "ctx", [(j, j + back) for j in range(n_ctx - back)])
            for back in range(1, reach + 1)
        ]
    )
    gathered = jnp.transpose(gather_fsdp(pieces, n_fsdp), (1, 0, 2, 3))
    keys_t = gathered[:, :key_devs].reshape(reach + 1, DH, tok_rows)
    values = jnp.transpose(gathered[:, key_devs:].reshape(reach + 1, DH, tok_rows), (0, 2, 1))
    return flash_attend(me, block_doc, q_rot, keys_t, values)


def solution(mesh):
    return jax.shard_map(
        on_device,
        mesh=mesh,
        in_specs=(P("ctx", "fsdp"), P("fsdp", None), P("fsdp", None), P()),
        out_specs=P("ctx", "fsdp"),
        check_vma=False,
    )
```

```python
import functools

import jax
import jax.numpy as jnp
from jax import lax
from jax.experimental import pallas as pl
from jax.experimental.layout import Layout, with_layout_constraint
from jax.experimental.pallas import tpu as pltpu
from jax.sharding import PartitionSpec as P

DH = 128
HQ = 16
BLOCK = 512
MAX_DOC_BLOCKS = 16


masked_low = -1e30


def frequencies():
    half_dim = DH // 2
    return 500000.0 ** (-2.0 * jnp.arange(half_dim, dtype=jnp.float32) / DH)


def rotate_pairs(vectors, positions):
    half_dim = DH // 2
    angles = positions[:, None].astype(jnp.float32) * frequencies()[None, :]
    cosine = jnp.cos(angles)
    sine = jnp.sin(angles)
    first_half = vectors[..., :half_dim]
    second_half = vectors[..., half_dim:]
    return jnp.concatenate(
        [first_half * cosine - second_half * sine, second_half * cosine + first_half * sine], -1
    )


def document_of(positions, block_doc):
    block_ids = positions // BLOCK
    table_ids = jnp.arange(block_doc.shape[0], dtype=jnp.int32)
    matches = block_ids[:, None] == table_ids[None, :]
    return jnp.sum(jnp.where(matches, block_doc[None, :], 0), axis=1)


def attend_tile(state_in, query_rows, query_pos, query_doc, key_rows, value_rows, key_pos, key_doc, valid):
    allowed = (key_pos[None, :] <= query_pos[:, None]) & (query_doc[:, None] == key_doc[None, :]) & valid
    scale = DH ** (-0.5)
    run_max, run_sum, run_out = state_in
    scores = (
        jnp.einsum("hqe,ke->hqk", query_rows, key_rows, preferred_element_type=jnp.float32) * scale
    )
    scores = jnp.where(allowed[None], scores, masked_low)
    new_max = jnp.maximum(run_max, jnp.max(scores, axis=-1))
    weights_f = jnp.where(allowed[None], jnp.exp(scores - new_max[..., None]), 0.0)
    rescale = jnp.exp(run_max - new_max)
    new_sum = run_sum * rescale + jnp.sum(weights_f, axis=-1)
    new_out = run_out * rescale[..., None] + jnp.einsum(
        "hqk,ke->hqe",
        weights_f.astype(jnp.bfloat16),
        value_rows,
        preferred_element_type=jnp.float32,
    )
    return (new_max, new_sum, new_out)


def flash_kernel(blocks_per_ctx, n_k, scalars, q_ref, k_ref, v_ref, o_ref, m_sc, l_sc, acc_sc):
    ki = pl.program_id(0)
    k_blk = scalars[1] + ki

    @pl.when(ki == 0)
    def _():
        m_sc[...] = jnp.full(m_sc.shape, masked_low, jnp.float32)
        l_sc[...] = jnp.zeros(l_sc.shape, jnp.float32)
        acc_sc[...] = jnp.zeros(acc_sc.shape, jnp.float32)

    def update(rows, diagonal):
        scale = DH ** (-0.5)
        scores = jnp.dot(q_ref[rows, :], k_ref[...], preferred_element_type=jnp.float32) * scale
        if diagonal:
            row_ids = lax.broadcasted_iota(jnp.int32, scores.shape, 0)
            col_ids = lax.broadcasted_iota(jnp.int32, scores.shape, 1)
            allowed = col_ids <= row_ids
            scores = jnp.where(allowed, scores, masked_low)
        m_prev = m_sc[rows, :]
        m_new = jnp.maximum(m_prev, jnp.max(scores, axis=1, keepdims=True))
        weights = jnp.exp(scores - m_new[:, :1])
        if diagonal:
            weights = jnp.where(allowed, weights, 0.0)
        rescale = jnp.exp(m_prev - m_new)
        l_sc[rows, :] = l_sc[rows, :] * rescale + jnp.sum(weights, axis=1, keepdims=True)
        acc_sc[rows, :] = acc_sc[rows, :] * rescale + jnp.dot(
            weights.astype(jnp.bfloat16), v_ref[...], preferred_element_type=jnp.float32
        )
        m_sc[rows, :] = m_new

    for sub in range(blocks_per_ctx):
        q_blk = scalars[0] * blocks_per_ctx + sub
        rows = pl.ds(sub * BLOCK, BLOCK)

        @pl.when((k_blk >= scalars[1 + sub]) & (k_blk < q_blk))
        def _():
            update(rows, False)

        @pl.when(k_blk == q_blk)
        def _():
            update(rows, True)

    @pl.when(ki == n_k - 1)
    def _():
        o_ref[...] = (acc_sc[...] / l_sc[...]).astype(o_ref.dtype)


def flash_attend(me, block_doc, q_rot, keys_t, values):
    n_back, _, tok_rows = keys_t.shape
    blocks_per_ctx = tok_rows // BLOCK
    n_k = min(MAX_DOC_BLOCKS + blocks_per_ctx - 1, n_back * blocks_per_ctx)
    q_blocks = me * blocks_per_ctx + jnp.arange(blocks_per_ctx, dtype=jnp.int32)
    first = jnp.sum(block_doc[None, :] < block_doc[q_blocks][:, None], axis=1).astype(jnp.int32)
    first = jnp.maximum(first, jnp.maximum(me - n_back + 1, 0) * blocks_per_ctx)
    scalars = jnp.concatenate([me.reshape(1).astype(jnp.int32), first])

    def key_block(ki, sc):
        blk = jnp.minimum(sc[1] + ki, sc[0] * blocks_per_ctx + blocks_per_ctx - 1)
        return sc[0] - blk // blocks_per_ctx, blk % blocks_per_ctx

    grid_spec = pltpu.PrefetchScalarGridSpec(
        num_scalar_prefetch=1,
        grid=(n_k,),
        in_specs=[
            pl.BlockSpec((tok_rows, DH), lambda ki, sc: (0, 0)),
            pl.BlockSpec((None, DH, BLOCK), lambda ki, sc: (key_block(ki, sc)[0], 0, key_block(ki, sc)[1])),
            pl.BlockSpec((None, BLOCK, DH), lambda ki, sc: key_block(ki, sc) + (0,)),
        ],
        out_specs=pl.BlockSpec((tok_rows, DH), lambda ki, sc: (0, 0)),
        scratch_shapes=[
            pltpu.VMEM((tok_rows, DH), jnp.float32),
            pltpu.VMEM((tok_rows, DH), jnp.float32),
            pltpu.VMEM((tok_rows, DH), jnp.float32),
        ],
    )
    return pl.pallas_call(
        functools.partial(flash_kernel, blocks_per_ctx, n_k),
        out_shape=jax.ShapeDtypeStruct((tok_rows, DH), jnp.bfloat16),
        grid_spec=grid_spec,
        compiler_params=pltpu.CompilerParams(dimension_semantics=("arbitrary",)),
        cost_estimate=pl.CostEstimate(
            flops=4 * BLOCK * BLOCK * DH * MAX_DOC_BLOCKS * blocks_per_ctx,
            transcendentals=BLOCK * BLOCK * MAX_DOC_BLOCKS * blocks_per_ctx,
            bytes_accessed=2 * BLOCK * 2 * DH * n_k + 4 * tok_rows * DH,
        ),
    )(scalars, q_rot, keys_t, values)


def gather_fsdp(piece, n_fsdp):
    me = lax.axis_index("fsdp")
    bits = n_fsdp.bit_length() - 1
    held = piece
    for bit in reversed(range(bits)):
        pairs = [(i, i ^ (1 << bit)) for i in range(n_fsdp)]
        theirs = lax.ppermute(held, "fsdp", pairs)
        mine_first = ((me >> bit) & 1) == 0
        held = jnp.where(mine_first, jnp.stack([held, theirs]), jnp.stack([theirs, held]))
    held = jnp.transpose(held, tuple(reversed(range(bits))) + tuple(range(bits, held.ndim)))
    return held.reshape((n_fsdp,) + piece.shape)


def on_device(hidden, w_query, w_key_value, block_doc):
    tok_rows, feat_rows = hidden.shape
    n_fsdp = lax.axis_size("fsdp")
    n_ctx = lax.axis_size("ctx")
    half_dim = DH // 2
    lanes = 128
    key_devs = n_fsdp // 2
    pairs = half_dim // key_devs
    rows = 2 * pairs
    w_keys = w_key_value[:, :DH]
    w_kv = jnp.concatenate(
        [
            jnp.concatenate(
                [
                    w_keys[:, :half_dim].reshape(feat_rows, key_devs, pairs),
                    w_keys[:, half_dim:].reshape(feat_rows, key_devs, pairs),
                ],
                axis=2,
            ),
            w_key_value[:, DH:].reshape(feat_rows, n_fsdp - key_devs, rows),
        ],
        axis=1,
    )
    hidden_rows = hidden.reshape(tok_rows // lanes, lanes, feat_rows)
    partial_kv = jnp.einsum("abd,dfc->fcab", hidden_rows, w_kv, preferred_element_type=jnp.float32)
    kv_sum = jnp.sum(lax.all_to_all(partial_kv, "fsdp", 0, 0, tiled=True), axis=0)
    kv_sum = kv_sum.reshape(rows, tok_rows)
    partial_q = jnp.einsum(
        "td,dfc->ftc", hidden, w_query.reshape(feat_rows, n_fsdp, DH), preferred_element_type=jnp.float32
    )
    partial_q = with_layout_constraint(partial_q, Layout(major_to_minor=(0, 1, 2)))
    q_sum = lax.psum_scatter(
        partial_q,
        "fsdp",
        scatter_dimension=0,
        tiled=True,
    )[0]
    me = lax.axis_index("ctx")
    me_f = lax.axis_index("fsdp")
    positions = me * tok_rows + jnp.arange(tok_rows, dtype=jnp.int32)
    q_rot = rotate_pairs(q_sum, positions).astype(jnp.bfloat16)
    q_rot = q_rot.reshape(tok_rows, 2, key_devs, pairs).transpose(0, 2, 1, 3).reshape(tok_rows, DH)
    key_a = kv_sum[:pairs]
    key_b = kv_sum[pairs:]
    freq = lax.dynamic_slice_in_dim(frequencies(), (me_f % key_devs) * pairs, pairs)
    k_angles = freq[:, None] * positions[None, :].astype(jnp.float32)
    k_cos = jnp.cos(k_angles)
    k_sin = jnp.sin(k_angles)
    rotated = jnp.concatenate([key_a * k_cos - key_b * k_sin, key_b * k_cos + key_a * k_sin], axis=0)
    piece = jnp.where(me_f < key_devs, rotated, kv_sum).astype(jnp.bfloat16)
    reach = min((MAX_DOC_BLOCKS * BLOCK - 1 + tok_rows - 1) // tok_rows, n_ctx - 1)
    pieces = jnp.stack(
        [piece]
        + [
            lax.ppermute(piece, "ctx", [(j, j + back) for j in range(n_ctx - back)])
            for back in range(1, reach + 1)
        ]
    )
    gathered = jnp.transpose(gather_fsdp(pieces, n_fsdp), (1, 0, 2, 3))
    keys_t = gathered[:, :key_devs].reshape(reach + 1, DH, tok_rows)
    values = jnp.transpose(gathered[:, key_devs:].reshape(reach + 1, DH, tok_rows), (0, 2, 1))
    return flash_attend(me, block_doc, q_rot, keys_t, values)


def solution(mesh):
    return jax.shard_map(
        on_device,
        mesh=mesh,
        in_specs=(P("ctx", "fsdp"), P("fsdp", None), P("fsdp", None), P()),
        out_specs=P("ctx", "fsdp"),
        check_vma=False,
    )
```

```python
import functools

import jax
import jax.numpy as jnp
from jax import lax
from jax.experimental import pallas as pl
from jax.experimental.layout import Layout, with_layout_constraint
from jax.experimental.pallas import tpu as pltpu
from jax.sharding import PartitionSpec as P

DH = 128
HQ = 16
BLOCK = 512
MAX_DOC_BLOCKS = 16


masked_low = -1e30


def frequencies():
    half_dim = DH // 2
    return 500000.0 ** (-2.0 * jnp.arange(half_dim, dtype=jnp.float32) / DH)


def rotate_pairs(vectors, positions):
    half_dim = DH // 2
    angles = positions[:, None].astype(jnp.float32) * frequencies()[None, :]
    cosine = jnp.cos(angles)
    sine = jnp.sin(angles)
    first_half = vectors[..., :half_dim]
    second_half = vectors[..., half_dim:]
    return jnp.concatenate(
        [first_half * cosine - second_half * sine, second_half * cosine + first_half * sine], -1
    )


def document_of(positions, block_doc):
    block_ids = positions // BLOCK
    table_ids = jnp.arange(block_doc.shape[0], dtype=jnp.int32)
    matches = block_ids[:, None] == table_ids[None, :]
    return jnp.sum(jnp.where(matches, block_doc[None, :], 0), axis=1)


def attend_tile(state_in, query_rows, query_pos, query_doc, key_rows, value_rows, key_pos, key_doc, valid):
    allowed = (key_pos[None, :] <= query_pos[:, None]) & (query_doc[:, None] == key_doc[None, :]) & valid
    scale = DH ** (-0.5)
    run_max, run_sum, run_out = state_in
    scores = (
        jnp.einsum("hqe,ke->hqk", query_rows, key_rows, preferred_element_type=jnp.float32) * scale
    )
    scores = jnp.where(allowed[None], scores, masked_low)
    new_max = jnp.maximum(run_max, jnp.max(scores, axis=-1))
    weights_f = jnp.where(allowed[None], jnp.exp(scores - new_max[..., None]), 0.0)
    rescale = jnp.exp(run_max - new_max)
    new_sum = run_sum * rescale + jnp.sum(weights_f, axis=-1)
    new_out = run_out * rescale[..., None] + jnp.einsum(
        "hqk,ke->hqe",
        weights_f.astype(jnp.bfloat16),
        value_rows,
        preferred_element_type=jnp.float32,
    )
    return (new_max, new_sum, new_out)


def flash_kernel(blocks_per_ctx, n_k, scalars, q_ref, k_ref, v_ref, o_ref, m_sc, l_sc, acc_sc):
    ki = pl.program_id(0)
    k_blk = scalars[1] + ki

    @pl.when(ki == 0)
    def _():
        m_sc[...] = jnp.full(m_sc.shape, masked_low, jnp.float32)
        l_sc[...] = jnp.zeros(l_sc.shape, jnp.float32)
        acc_sc[...] = jnp.zeros(acc_sc.shape, jnp.float32)

    def update(rows, diagonal):
        scale = DH ** (-0.5)
        scores = jnp.dot(q_ref[rows, :], k_ref[...], preferred_element_type=jnp.float32) * scale
        if diagonal:
            row_ids = lax.broadcasted_iota(jnp.int32, scores.shape, 0)
            col_ids = lax.broadcasted_iota(jnp.int32, scores.shape, 1)
            allowed = col_ids <= row_ids
            scores = jnp.where(allowed, scores, masked_low)
        m_prev = m_sc[rows, :]
        m_new = jnp.maximum(m_prev, jnp.max(scores, axis=1, keepdims=True))
        weights = jnp.exp(scores - m_new[:, :1])
        if diagonal:
            weights = jnp.where(allowed, weights, 0.0)
        rescale = jnp.exp(m_prev - m_new)
        l_sc[rows, :] = l_sc[rows, :] * rescale + jnp.sum(weights, axis=1, keepdims=True)
        acc_sc[rows, :] = acc_sc[rows, :] * rescale + jnp.dot(
            weights.astype(jnp.bfloat16), v_ref[...], preferred_element_type=jnp.float32
        )
        m_sc[rows, :] = m_new

    for sub in range(blocks_per_ctx):
        q_blk = scalars[0] * blocks_per_ctx + sub
        rows = pl.ds(sub * BLOCK, BLOCK)

        @pl.when((k_blk >= scalars[1 + sub]) & (k_blk < q_blk))
        def _():
            update(rows, False)

        @pl.when(k_blk == q_blk)
        def _():
            update(rows, True)

    @pl.when(ki == n_k - 1)
    def _():
        o_ref[...] = (acc_sc[...] / l_sc[...]).astype(o_ref.dtype)


def flash_attend(me, block_doc, q_rot, keys_t, values):
    n_back, _, tok_rows = keys_t.shape
    blocks_per_ctx = tok_rows // BLOCK
    n_k = min(MAX_DOC_BLOCKS + blocks_per_ctx - 1, n_back * blocks_per_ctx)
    q_blocks = me * blocks_per_ctx + jnp.arange(blocks_per_ctx, dtype=jnp.int32)
    first = jnp.sum(block_doc[None, :] < block_doc[q_blocks][:, None], axis=1).astype(jnp.int32)
    first = jnp.maximum(first, jnp.maximum(me - n_back + 1, 0) * blocks_per_ctx)
    scalars = jnp.concatenate([me.reshape(1).astype(jnp.int32), first])

    def key_block(ki, sc):
        blk = jnp.minimum(sc[1] + ki, sc[0] * blocks_per_ctx + blocks_per_ctx - 1)
        return sc[0] - blk // blocks_per_ctx, blk % blocks_per_ctx

    grid_spec = pltpu.PrefetchScalarGridSpec(
        num_scalar_prefetch=1,
        grid=(n_k,),
        in_specs=[
            pl.BlockSpec((tok_rows, DH), lambda ki, sc: (0, 0)),
            pl.BlockSpec((None, DH, BLOCK), lambda ki, sc: (key_block(ki, sc)[0], 0, key_block(ki, sc)[1])),
            pl.BlockSpec((None, BLOCK, DH), lambda ki, sc: key_block(ki, sc) + (0,)),
        ],
        out_specs=pl.BlockSpec((tok_rows, DH), lambda ki, sc: (0, 0)),
        scratch_shapes=[
            pltpu.VMEM((tok_rows, DH), jnp.float32),
            pltpu.VMEM((tok_rows, DH), jnp.float32),
            pltpu.VMEM((tok_rows, DH), jnp.float32),
        ],
    )
    return pl.pallas_call(
        functools.partial(flash_kernel, blocks_per_ctx, n_k),
        out_shape=jax.ShapeDtypeStruct((tok_rows, DH), jnp.bfloat16),
        grid_spec=grid_spec,
        compiler_params=pltpu.CompilerParams(dimension_semantics=("arbitrary",)),
        cost_estimate=pl.CostEstimate(
            flops=4 * BLOCK * BLOCK * DH * MAX_DOC_BLOCKS * blocks_per_ctx,
            transcendentals=BLOCK * BLOCK * MAX_DOC_BLOCKS * blocks_per_ctx,
            bytes_accessed=2 * BLOCK * 2 * DH * n_k + 4 * tok_rows * DH,
        ),
    )(scalars, q_rot, keys_t, values)


def gather_fsdp(piece, n_fsdp):
    me = lax.axis_index("fsdp")
    bits = n_fsdp.bit_length() - 1
    held = piece
    for bit in reversed(range(bits)):
        pairs = [(i, i ^ (1 << bit)) for i in range(n_fsdp)]
        theirs = lax.ppermute(held, "fsdp", pairs)
        mine_first = ((me >> bit) & 1) == 0
        held = jnp.where(mine_first, jnp.stack([held, theirs]), jnp.stack([theirs, held]))
    held = jnp.transpose(held, tuple(reversed(range(bits))) + tuple(range(bits, held.ndim)))
    return held.reshape((n_fsdp,) + piece.shape)


def on_device(hidden, w_query, w_key_value, block_doc):
    tok_rows, feat_rows = hidden.shape
    n_fsdp = lax.axis_size("fsdp")
    n_ctx = lax.axis_size("ctx")
    half_dim = DH // 2
    lanes = 128
    key_devs = n_fsdp // 2
    pairs = half_dim // key_devs
    rows = 2 * pairs
    w_keys = w_key_value[:, :DH]
    w_kv = jnp.concatenate(
        [
            jnp.concatenate(
                [
                    w_keys[:, :half_dim].reshape(feat_rows, key_devs, pairs),
                    w_keys[:, half_dim:].reshape(feat_rows, key_devs, pairs),
                ],
                axis=2,
            ),
            w_key_value[:, DH:].reshape(feat_rows, n_fsdp - key_devs, rows),
        ],
        axis=1,
    )
    hidden_rows = hidden.reshape(tok_rows // lanes, lanes, feat_rows)
    partial_kv = jnp.einsum("abd,dfc->fcab", hidden_rows, w_kv, preferred_element_type=jnp.float32)
    kv_sum = jnp.sum(lax.all_to_all(partial_kv, "fsdp", 0, 0, tiled=True), axis=0)
    kv_sum = kv_sum.reshape(rows, tok_rows)
    partial_q = jnp.einsum(
        "td,dfc->ftc", hidden, w_query.reshape(feat_rows, n_fsdp, DH), preferred_element_type=jnp.float32
    )
    partial_q = with_layout_constraint(partial_q, Layout(major_to_minor=(0, 1, 2)))
    q_sum = lax.psum_scatter(
        partial_q,
        "fsdp",
        scatter_dimension=0,
        tiled=True,
    )[0]
    me = lax.axis_index("ctx")
    me_f = lax.axis_index("fsdp")
    positions = me * tok_rows + jnp.arange(tok_rows, dtype=jnp.int32)
    q_rot = rotate_pairs(q_sum, positions).astype(jnp.bfloat16)
    key_a = kv_sum[:pairs]
    key_b = kv_sum[pairs:]
    freq = lax.dynamic_slice_in_dim(frequencies(), (me_f % key_devs) * pairs, pairs)
    k_angles = freq[:, None] * positions[None, :].astype(jnp.float32)
    k_cos = jnp.cos(k_angles)
    k_sin = jnp.sin(k_angles)
    rotated = jnp.concatenate([key_a * k_cos - key_b * k_sin, key_b * k_cos + key_a * k_sin], axis=0)
    piece = jnp.where(me_f < key_devs, rotated, kv_sum).astype(jnp.bfloat16)
    reach = min((MAX_DOC_BLOCKS * BLOCK - 1 + tok_rows - 1) // tok_rows, n_ctx - 1)
    pieces = jnp.stack(
        [piece]
        + [
            lax.ppermute(piece, "ctx", [(j, j + back) for j in range(n_ctx - back)])
            for back in range(1, reach + 1)
        ]
    )
    gathered = jnp.transpose(gather_fsdp(pieces, n_fsdp), (1, 0, 2, 3))
    keys_t = gathered[:, :key_devs].reshape(reach + 1, key_devs, 2, pairs, tok_rows)
    keys_t = keys_t.transpose(0, 2, 1, 3, 4).reshape(reach + 1, DH, tok_rows)
    values = jnp.transpose(gathered[:, key_devs:].reshape(reach + 1, DH, tok_rows), (0, 2, 1))
    return flash_attend(me, block_doc, q_rot, keys_t, values)


def solution(mesh):
    return jax.shard_map(
        on_device,
        mesh=mesh,
        in_specs=(P("ctx", "fsdp"), P("fsdp", None), P("fsdp", None), P()),
        out_specs=P("ctx", "fsdp"),
        check_vma=False,
    )
```

```python
import functools

import jax
import jax.numpy as jnp
from jax import lax
from jax.experimental import pallas as pl
from jax.experimental.layout import Layout, with_layout_constraint
from jax.experimental.pallas import tpu as pltpu
from jax.sharding import PartitionSpec as P

DH = 128
HQ = 16
BLOCK = 512
MAX_DOC_BLOCKS = 16


masked_low = -1e30


def frequencies():
    half_dim = DH // 2
    return 500000.0 ** (-2.0 * jnp.arange(half_dim, dtype=jnp.float32) / DH)


def rotate_pairs(vectors, positions):
    half_dim = DH // 2
    angles = positions[:, None].astype(jnp.float32) * frequencies()[None, :]
    cosine = jnp.cos(angles)
    sine = jnp.sin(angles)
    first_half = vectors[..., :half_dim]
    second_half = vectors[..., half_dim:]
    return jnp.concatenate(
        [first_half * cosine - second_half * sine, second_half * cosine + first_half * sine], -1
    )


def document_of(positions, block_doc):
    block_ids = positions // BLOCK
    table_ids = jnp.arange(block_doc.shape[0], dtype=jnp.int32)
    matches = block_ids[:, None] == table_ids[None, :]
    return jnp.sum(jnp.where(matches, block_doc[None, :], 0), axis=1)


def attend_tile(state_in, query_rows, query_pos, query_doc, key_rows, value_rows, key_pos, key_doc, valid):
    allowed = (key_pos[None, :] <= query_pos[:, None]) & (query_doc[:, None] == key_doc[None, :]) & valid
    scale = DH ** (-0.5)
    run_max, run_sum, run_out = state_in
    scores = (
        jnp.einsum("hqe,ke->hqk", query_rows, key_rows, preferred_element_type=jnp.float32) * scale
    )
    scores = jnp.where(allowed[None], scores, masked_low)
    new_max = jnp.maximum(run_max, jnp.max(scores, axis=-1))
    weights_f = jnp.where(allowed[None], jnp.exp(scores - new_max[..., None]), 0.0)
    rescale = jnp.exp(run_max - new_max)
    new_sum = run_sum * rescale + jnp.sum(weights_f, axis=-1)
    new_out = run_out * rescale[..., None] + jnp.einsum(
        "hqk,ke->hqe",
        weights_f.astype(jnp.bfloat16),
        value_rows,
        preferred_element_type=jnp.float32,
    )
    return (new_max, new_sum, new_out)


def flash_kernel(blocks_per_ctx, n_k, scalars, q_ref, cos_ref, sin_ref, k_ref, v_ref, o_ref, m_sc, l_sc, acc_sc, q_sc):
    ki = pl.program_id(0)

    @pl.when(ki == 0)
    def _():
        query = q_ref[...]
        swapped = pltpu.roll(query, DH // 2, 1)
        q_sc[...] = (query * cos_ref[...] + swapped * sin_ref[...]).astype(q_sc.dtype)
    k_blk = scalars[1] + ki

    @pl.when(ki == 0)
    def _():
        m_sc[...] = jnp.full(m_sc.shape, masked_low, jnp.float32)
        l_sc[...] = jnp.zeros(l_sc.shape, jnp.float32)
        acc_sc[...] = jnp.zeros(acc_sc.shape, jnp.float32)

    def update(rows, diagonal):
        scale = DH ** (-0.5)
        scores = jnp.dot(q_sc[rows, :], k_ref[...], preferred_element_type=jnp.float32) * scale
        if diagonal:
            row_ids = lax.broadcasted_iota(jnp.int32, scores.shape, 0)
            col_ids = lax.broadcasted_iota(jnp.int32, scores.shape, 1)
            allowed = col_ids <= row_ids
            scores = jnp.where(allowed, scores, masked_low)
        m_prev = m_sc[rows, :]
        m_new = jnp.maximum(m_prev, jnp.max(scores, axis=1, keepdims=True))
        weights = jnp.exp(scores - m_new[:, :1])
        if diagonal:
            weights = jnp.where(allowed, weights, 0.0)
        rescale = jnp.exp(m_prev - m_new)
        l_sc[rows, :] = l_sc[rows, :] * rescale + jnp.sum(weights, axis=1, keepdims=True)
        acc_sc[rows, :] = acc_sc[rows, :] * rescale + jnp.dot(
            weights.astype(jnp.bfloat16), v_ref[...], preferred_element_type=jnp.float32
        )
        m_sc[rows, :] = m_new

    for sub in range(blocks_per_ctx):
        q_blk = scalars[0] * blocks_per_ctx + sub
        rows = pl.ds(sub * BLOCK, BLOCK)

        @pl.when((k_blk >= scalars[1 + sub]) & (k_blk < q_blk))
        def _():
            update(rows, False)

        @pl.when(k_blk == q_blk)
        def _():
            update(rows, True)

    @pl.when(ki == n_k - 1)
    def _():
        o_ref[...] = (acc_sc[...] / l_sc[...]).astype(o_ref.dtype)


def flash_attend(me, block_doc, q_sum, cos_t, sin_t, keys_t, values):
    n_back, _, tok_rows = keys_t.shape
    blocks_per_ctx = tok_rows // BLOCK
    n_k = min(MAX_DOC_BLOCKS + blocks_per_ctx - 1, n_back * blocks_per_ctx)
    q_blocks = me * blocks_per_ctx + jnp.arange(blocks_per_ctx, dtype=jnp.int32)
    first = jnp.sum(block_doc[None, :] < block_doc[q_blocks][:, None], axis=1).astype(jnp.int32)
    first = jnp.maximum(first, jnp.maximum(me - n_back + 1, 0) * blocks_per_ctx)
    scalars = jnp.concatenate([me.reshape(1).astype(jnp.int32), first])

    def key_block(ki, sc):
        blk = jnp.minimum(sc[1] + ki, sc[0] * blocks_per_ctx + blocks_per_ctx - 1)
        return sc[0] - blk // blocks_per_ctx, blk % blocks_per_ctx

    grid_spec = pltpu.PrefetchScalarGridSpec(
        num_scalar_prefetch=1,
        grid=(n_k,),
        in_specs=[
            pl.BlockSpec((tok_rows, DH), lambda ki, sc: (0, 0)),
            pl.BlockSpec((tok_rows, DH), lambda ki, sc: (0, 0)),
            pl.BlockSpec((tok_rows, DH), lambda ki, sc: (0, 0)),
            pl.BlockSpec((None, DH, BLOCK), lambda ki, sc: (key_block(ki, sc)[0], 0, key_block(ki, sc)[1])),
            pl.BlockSpec((None, BLOCK, DH), lambda ki, sc: key_block(ki, sc) + (0,)),
        ],
        out_specs=pl.BlockSpec((tok_rows, DH), lambda ki, sc: (0, 0)),
        scratch_shapes=[
            pltpu.VMEM((tok_rows, DH), jnp.float32),
            pltpu.VMEM((tok_rows, DH), jnp.float32),
            pltpu.VMEM((tok_rows, DH), jnp.float32),
            pltpu.VMEM((tok_rows, DH), jnp.bfloat16),
        ],
    )
    return pl.pallas_call(
        functools.partial(flash_kernel, blocks_per_ctx, n_k),
        out_shape=jax.ShapeDtypeStruct((tok_rows, DH), jnp.bfloat16),
        grid_spec=grid_spec,
        compiler_params=pltpu.CompilerParams(dimension_semantics=("arbitrary",)),
        cost_estimate=pl.CostEstimate(
            flops=4 * BLOCK * BLOCK * DH * MAX_DOC_BLOCKS * blocks_per_ctx,
            transcendentals=BLOCK * BLOCK * MAX_DOC_BLOCKS * blocks_per_ctx,
            bytes_accessed=2 * BLOCK * 2 * DH * n_k + 4 * tok_rows * DH,
        ),
    )(scalars, q_sum, cos_t, sin_t, keys_t, values)


def gather_fsdp(piece, n_fsdp):
    me = lax.axis_index("fsdp")
    bits = n_fsdp.bit_length() - 1
    held = piece
    for bit in reversed(range(bits)):
        pairs = [(i, i ^ (1 << bit)) for i in range(n_fsdp)]
        theirs = lax.ppermute(held, "fsdp", pairs)
        mine_first = ((me >> bit) & 1) == 0
        held = jnp.where(mine_first, jnp.stack([held, theirs]), jnp.stack([theirs, held]))
    held = jnp.transpose(held, tuple(reversed(range(bits))) + tuple(range(bits, held.ndim)))
    return held.reshape((n_fsdp,) + piece.shape)


def on_device(hidden, w_query, w_key_value, block_doc):
    tok_rows, feat_rows = hidden.shape
    n_fsdp = lax.axis_size("fsdp")
    n_ctx = lax.axis_size("ctx")
    half_dim = DH // 2
    lanes = 128
    key_devs = n_fsdp // 2
    pairs = half_dim // key_devs
    rows = 2 * pairs
    w_keys = w_key_value[:, :DH]
    w_kv = jnp.concatenate(
        [
            jnp.concatenate(
                [
                    w_keys[:, :half_dim].reshape(feat_rows, key_devs, pairs),
                    w_keys[:, half_dim:].reshape(feat_rows, key_devs, pairs),
                ],
                axis=2,
            ),
            w_key_value[:, DH:].reshape(feat_rows, n_fsdp - key_devs, rows),
        ],
        axis=1,
    )
    hidden_rows = hidden.reshape(tok_rows // lanes, lanes, feat_rows)
    partial_kv = jnp.einsum("abd,dfc->fcab", hidden_rows, w_kv, preferred_element_type=jnp.float32)
    kv_sum = jnp.sum(lax.all_to_all(partial_kv, "fsdp", 0, 0, tiled=True), axis=0)
    kv_sum = kv_sum.reshape(rows, tok_rows)
    partial_q = jnp.einsum(
        "td,dfc->ftc", hidden, w_query.reshape(feat_rows, n_fsdp, DH), preferred_element_type=jnp.float32
    )
    partial_q = with_layout_constraint(partial_q, Layout(major_to_minor=(0, 1, 2)))
    q_sum = lax.psum_scatter(
        partial_q,
        "fsdp",
        scatter_dimension=0,
        tiled=True,
    )[0]
    me = lax.axis_index("ctx")
    me_f = lax.axis_index("fsdp")
    positions = me * tok_rows + jnp.arange(tok_rows, dtype=jnp.int32)
    q_angles = positions[:, None].astype(jnp.float32) * frequencies()[None, :]
    q_cos = jnp.cos(q_angles)
    q_sin = jnp.sin(q_angles)
    cos_t = jnp.concatenate([q_cos, q_cos], axis=1)
    sin_t = jnp.concatenate([-q_sin, q_sin], axis=1)
    key_a = kv_sum[:pairs]
    key_b = kv_sum[pairs:]
    freq = lax.dynamic_slice_in_dim(frequencies(), (me_f % key_devs) * pairs, pairs)
    k_angles = freq[:, None] * positions[None, :].astype(jnp.float32)
    k_cos = jnp.cos(k_angles)
    k_sin = jnp.sin(k_angles)
    rotated = jnp.concatenate([key_a * k_cos - key_b * k_sin, key_b * k_cos + key_a * k_sin], axis=0)
    piece = jnp.where(me_f < key_devs, rotated, kv_sum).astype(jnp.bfloat16)
    reach = min((MAX_DOC_BLOCKS * BLOCK - 1 + tok_rows - 1) // tok_rows, n_ctx - 1)
    pieces = jnp.stack(
        [piece]
        + [
            lax.ppermute(piece, "ctx", [(j, j + back) for j in range(n_ctx - back)])
            for back in range(1, reach + 1)
        ]
    )
    gathered = jnp.transpose(gather_fsdp(pieces, n_fsdp), (1, 0, 2, 3))
    keys_t = gathered[:, :key_devs].reshape(reach + 1, key_devs, 2, pairs, tok_rows)
    keys_t = keys_t.transpose(0, 2, 1, 3, 4).reshape(reach + 1, DH, tok_rows)
    values = jnp.transpose(gathered[:, key_devs:].reshape(reach + 1, DH, tok_rows), (0, 2, 1))
    return flash_attend(me, block_doc, q_sum, cos_t, sin_t, keys_t, values)


def solution(mesh):
    return jax.shard_map(
        on_device,
        mesh=mesh,
        in_specs=(P("ctx", "fsdp"), P("fsdp", None), P("fsdp", None), P()),
        out_specs=P("ctx", "fsdp"),
        check_vma=False,
    )
```

```python
import functools

import jax
import jax.numpy as jnp
from jax import lax
from jax.experimental import pallas as pl
from jax.experimental.layout import Layout, with_layout_constraint
from jax.experimental.pallas import tpu as pltpu
from jax.sharding import PartitionSpec as P

DH = 128
HQ = 16
BLOCK = 512
MAX_DOC_BLOCKS = 16


masked_low = -1e30


def frequencies():
    half_dim = DH // 2
    return 500000.0 ** (-2.0 * jnp.arange(half_dim, dtype=jnp.float32) / DH)


def rotate_pairs(vectors, positions):
    half_dim = DH // 2
    angles = positions[:, None].astype(jnp.float32) * frequencies()[None, :]
    cosine = jnp.cos(angles)
    sine = jnp.sin(angles)
    first_half = vectors[..., :half_dim]
    second_half = vectors[..., half_dim:]
    return jnp.concatenate(
        [first_half * cosine - second_half * sine, second_half * cosine + first_half * sine], -1
    )


def document_of(positions, block_doc):
    block_ids = positions // BLOCK
    table_ids = jnp.arange(block_doc.shape[0], dtype=jnp.int32)
    matches = block_ids[:, None] == table_ids[None, :]
    return jnp.sum(jnp.where(matches, block_doc[None, :], 0), axis=1)


def attend_tile(state_in, query_rows, query_pos, query_doc, key_rows, value_rows, key_pos, key_doc, valid):
    allowed = (key_pos[None, :] <= query_pos[:, None]) & (query_doc[:, None] == key_doc[None, :]) & valid
    scale = DH ** (-0.5)
    run_max, run_sum, run_out = state_in
    scores = (
        jnp.einsum("hqe,ke->hqk", query_rows, key_rows, preferred_element_type=jnp.float32) * scale
    )
    scores = jnp.where(allowed[None], scores, masked_low)
    new_max = jnp.maximum(run_max, jnp.max(scores, axis=-1))
    weights_f = jnp.where(allowed[None], jnp.exp(scores - new_max[..., None]), 0.0)
    rescale = jnp.exp(run_max - new_max)
    new_sum = run_sum * rescale + jnp.sum(weights_f, axis=-1)
    new_out = run_out * rescale[..., None] + jnp.einsum(
        "hqk,ke->hqe",
        weights_f.astype(jnp.bfloat16),
        value_rows,
        preferred_element_type=jnp.float32,
    )
    return (new_max, new_sum, new_out)


def flash_kernel(blocks_per_ctx, n_k, scalars, q_ref, cos_ref, sin_ref, k_ref, v_ref, o_ref, m_sc, l_sc, acc_sc, q_sc):
    ki = pl.program_id(0)

    @pl.when(ki == 0)
    def _():
        query = q_ref[...]
        swapped = pltpu.roll(query, DH // 2, 1)
        q_sc[...] = (query * cos_ref[...] + swapped * sin_ref[...]).astype(q_sc.dtype)
    k_blk = scalars[1] + ki

    @pl.when(ki == 0)
    def _():
        m_sc[...] = jnp.full(m_sc.shape, masked_low, jnp.float32)
        l_sc[...] = jnp.zeros(l_sc.shape, jnp.float32)
        acc_sc[...] = jnp.zeros(acc_sc.shape, jnp.float32)

    def update(rows, diagonal):
        scale = DH ** (-0.5)
        scores = jnp.dot(q_sc[rows, :], k_ref[...], preferred_element_type=jnp.float32) * scale
        if diagonal:
            row_ids = lax.broadcasted_iota(jnp.int32, scores.shape, 0)
            col_ids = lax.broadcasted_iota(jnp.int32, scores.shape, 1)
            allowed = col_ids <= row_ids
            scores = jnp.where(allowed, scores, masked_low)
        m_prev = m_sc[rows, :]
        m_new = jnp.maximum(m_prev, jnp.max(scores, axis=1, keepdims=True))
        weights = jnp.exp(scores - m_new[:, :1])
        if diagonal:
            weights = jnp.where(allowed, weights, 0.0)
        rescale = jnp.exp(m_prev - m_new)
        weights_b = weights.astype(jnp.bfloat16)
        ones = jnp.ones((weights.shape[1], DH), jnp.bfloat16)
        l_sc[rows, :] = l_sc[rows, :] * rescale + jnp.dot(weights_b, ones, preferred_element_type=jnp.float32)
        acc_sc[rows, :] = acc_sc[rows, :] * rescale + jnp.dot(
            weights_b, v_ref[...], preferred_element_type=jnp.float32
        )
        m_sc[rows, :] = m_new

    for sub in range(blocks_per_ctx):
        q_blk = scalars[0] * blocks_per_ctx + sub
        rows = pl.ds(sub * BLOCK, BLOCK)

        @pl.when((k_blk >= scalars[1 + sub]) & (k_blk < q_blk))
        def _():
            update(rows, False)

        @pl.when(k_blk == q_blk)
        def _():
            update(rows, True)

    @pl.when(ki == n_k - 1)
    def _():
        o_ref[...] = (acc_sc[...] / l_sc[...]).astype(o_ref.dtype)


def flash_attend(me, block_doc, q_sum, cos_t, sin_t, keys_t, values):
    n_back, _, tok_rows = keys_t.shape
    blocks_per_ctx = tok_rows // BLOCK
    n_k = min(MAX_DOC_BLOCKS + blocks_per_ctx - 1, n_back * blocks_per_ctx)
    q_blocks = me * blocks_per_ctx + jnp.arange(blocks_per_ctx, dtype=jnp.int32)
    first = jnp.sum(block_doc[None, :] < block_doc[q_blocks][:, None], axis=1).astype(jnp.int32)
    first = jnp.maximum(first, jnp.maximum(me - n_back + 1, 0) * blocks_per_ctx)
    scalars = jnp.concatenate([me.reshape(1).astype(jnp.int32), first])

    def key_block(ki, sc):
        blk = jnp.minimum(sc[1] + ki, sc[0] * blocks_per_ctx + blocks_per_ctx - 1)
        return sc[0] - blk // blocks_per_ctx, blk % blocks_per_ctx

    grid_spec = pltpu.PrefetchScalarGridSpec(
        num_scalar_prefetch=1,
        grid=(n_k,),
        in_specs=[
            pl.BlockSpec((tok_rows, DH), lambda ki, sc: (0, 0)),
            pl.BlockSpec((tok_rows, DH), lambda ki, sc: (0, 0)),
            pl.BlockSpec((tok_rows, DH), lambda ki, sc: (0, 0)),
            pl.BlockSpec((None, DH, BLOCK), lambda ki, sc: (key_block(ki, sc)[0], 0, key_block(ki, sc)[1])),
            pl.BlockSpec((None, BLOCK, DH), lambda ki, sc: key_block(ki, sc) + (0,)),
        ],
        out_specs=pl.BlockSpec((tok_rows, DH), lambda ki, sc: (0, 0)),
        scratch_shapes=[
            pltpu.VMEM((tok_rows, DH), jnp.float32),
            pltpu.VMEM((tok_rows, DH), jnp.float32),
            pltpu.VMEM((tok_rows, DH), jnp.float32),
            pltpu.VMEM((tok_rows, DH), jnp.bfloat16),
        ],
    )
    return pl.pallas_call(
        functools.partial(flash_kernel, blocks_per_ctx, n_k),
        out_shape=jax.ShapeDtypeStruct((tok_rows, DH), jnp.bfloat16),
        grid_spec=grid_spec,
        compiler_params=pltpu.CompilerParams(dimension_semantics=("arbitrary",)),
        cost_estimate=pl.CostEstimate(
            flops=4 * BLOCK * BLOCK * DH * MAX_DOC_BLOCKS * blocks_per_ctx,
            transcendentals=BLOCK * BLOCK * MAX_DOC_BLOCKS * blocks_per_ctx,
            bytes_accessed=2 * BLOCK * 2 * DH * n_k + 4 * tok_rows * DH,
        ),
    )(scalars, q_sum, cos_t, sin_t, keys_t, values)


def gather_fsdp(piece, n_fsdp):
    me = lax.axis_index("fsdp")
    bits = n_fsdp.bit_length() - 1
    held = piece
    for bit in reversed(range(bits)):
        pairs = [(i, i ^ (1 << bit)) for i in range(n_fsdp)]
        theirs = lax.ppermute(held, "fsdp", pairs)
        mine_first = ((me >> bit) & 1) == 0
        held = jnp.where(mine_first, jnp.stack([held, theirs]), jnp.stack([theirs, held]))
    held = jnp.transpose(held, tuple(reversed(range(bits))) + tuple(range(bits, held.ndim)))
    return held.reshape((n_fsdp,) + piece.shape)


def on_device(hidden, w_query, w_key_value, block_doc):
    tok_rows, feat_rows = hidden.shape
    n_fsdp = lax.axis_size("fsdp")
    n_ctx = lax.axis_size("ctx")
    half_dim = DH // 2
    lanes = 128
    key_devs = n_fsdp // 2
    pairs = half_dim // key_devs
    rows = 2 * pairs
    w_keys = w_key_value[:, :DH]
    w_kv = jnp.concatenate(
        [
            jnp.concatenate(
                [
                    w_keys[:, :half_dim].reshape(feat_rows, key_devs, pairs),
                    w_keys[:, half_dim:].reshape(feat_rows, key_devs, pairs),
                ],
                axis=2,
            ),
            w_key_value[:, DH:].reshape(feat_rows, n_fsdp - key_devs, rows),
        ],
        axis=1,
    )
    hidden_rows = hidden.reshape(tok_rows // lanes, lanes, feat_rows)
    partial_kv = jnp.einsum("abd,dfc->fcab", hidden_rows, w_kv, preferred_element_type=jnp.float32)
    kv_sum = jnp.sum(lax.all_to_all(partial_kv, "fsdp", 0, 0, tiled=True), axis=0)
    kv_sum = kv_sum.reshape(rows, tok_rows)
    partial_q = jnp.einsum(
        "td,dfc->ftc", hidden, w_query.reshape(feat_rows, n_fsdp, DH), preferred_element_type=jnp.float32
    )
    partial_q = with_layout_constraint(partial_q, Layout(major_to_minor=(0, 1, 2)))
    q_sum = lax.psum_scatter(
        partial_q,
        "fsdp",
        scatter_dimension=0,
        tiled=True,
    )[0]
    me = lax.axis_index("ctx")
    me_f = lax.axis_index("fsdp")
    positions = me * tok_rows + jnp.arange(tok_rows, dtype=jnp.int32)
    q_angles = positions[:, None].astype(jnp.float32) * frequencies()[None, :]
    q_cos = jnp.cos(q_angles)
    q_sin = jnp.sin(q_angles)
    cos_t = jnp.concatenate([q_cos, q_cos], axis=1)
    sin_t = jnp.concatenate([-q_sin, q_sin], axis=1)
    key_a = kv_sum[:pairs]
    key_b = kv_sum[pairs:]
    freq = lax.dynamic_slice_in_dim(frequencies(), (me_f % key_devs) * pairs, pairs)
    k_angles = freq[:, None] * positions[None, :].astype(jnp.float32)
    k_cos = jnp.cos(k_angles)
    k_sin = jnp.sin(k_angles)
    rotated = jnp.concatenate([key_a * k_cos - key_b * k_sin, key_b * k_cos + key_a * k_sin], axis=0)
    piece = jnp.where(me_f < key_devs, rotated, kv_sum).astype(jnp.bfloat16)
    reach = min((MAX_DOC_BLOCKS * BLOCK - 1 + tok_rows - 1) // tok_rows, n_ctx - 1)
    pieces = jnp.stack(
        [piece]
        + [
            lax.ppermute(piece, "ctx", [(j, j + back) for j in range(n_ctx - back)])
            for back in range(1, reach + 1)
        ]
    )
    gathered = jnp.transpose(gather_fsdp(pieces, n_fsdp), (1, 0, 2, 3))
    keys_t = gathered[:, :key_devs].reshape(reach + 1, key_devs, 2, pairs, tok_rows)
    keys_t = keys_t.transpose(0, 2, 1, 3, 4).reshape(reach + 1, DH, tok_rows)
    values = jnp.transpose(gathered[:, key_devs:].reshape(reach + 1, DH, tok_rows), (0, 2, 1))
    return flash_attend(me, block_doc, q_sum, cos_t, sin_t, keys_t, values)


def solution(mesh):
    return jax.shard_map(
        on_device,
        mesh=mesh,
        in_specs=(P("ctx", "fsdp"), P("fsdp", None), P("fsdp", None), P()),
        out_specs=P("ctx", "fsdp"),
        check_vma=False,
    )
```
